128 devices in a mesh: blk: 16 (over z, y), exp: 8 (over x, core).
Axes of the slice: x: 4, y: 4, z: 4, core: 2. Of those that a mesh axis runs over, the one named last changes fastest.
Arguments:
- stream: bfloat16 [16384, 2048], P(('blk', 'exp')), may hold values from -6 to 6
- norm_gain: float32 [2048], replicated, may hold values from 0.5 to 1.5
- query_weight: bfloat16 [2048, 1024], P(None, 'exp')
- key_weight: bfloat16 [2048, 1024], P(None, 'exp')
- value_weight: bfloat16 [2048, 1024], P(None, 'exp'), may hold values from -0.125 to 0.125
- output_weight: bfloat16 [1024, 2048], replicated, may hold values from -0.1875 to 0.1875
- post_gain: float32 [2048], replicated, may hold values from 0.5 to 1.5
- shared_gate: bfloat16 [2048, 3072], P(None, 'exp'), may hold values from -0.125 to 0.125
- shared_up: bfloat16 [2048, 3072], P(None, 'exp'), may hold values from -0.125 to 0.125
- shared_down: bfloat16 [3072, 2048], P('exp'), may hold values from -0.109375 to 0.109375
- shared_router: bfloat16 [2048], replicated, may hold values from -0.125 to 0.125
- expert_gate: bfloat16 [128, 2048, 704], P(('blk', 'exp')), may hold values from -0.125 to 0.125
- expert_up: bfloat16 [128, 2048, 704], P(('blk', 'exp')), may hold values from -0.125 to 0.125
- expert_down: bfloat16 [128, 704, 2048], P(('blk', 'exp')), may hold values from -0.15625 to 0.15625
- expert_ids: int32 [16384, 4], P(('blk', 'exp')), may hold values from 0 to 63, all different within a row; in each aligned block of 128 rows (0 to 127, 128 to 255, ...) at most 10 rows name the same one
- route_weights: float32 [16384, 4], P(('blk', 'exp')), may hold values from 0.05 to 0.5
- positions: int32 [16384], P(('blk', 'exp')), may hold values from 0 to 16383, as said below
- segment_ids: int32 [16384], P(('blk', 'exp')), may hold values from 0 to 11, as said below
- cache_slots: int32 [16384], P(('blk', 'exp')), may hold values from 0 to 1023, as said below
Outputs:
- final: bfloat16 [16384, 2048], P(('blk', 'exp'))
- cache_keys: bfloat16 [16384, 1024], P('blk', 'exp')
- cache_values: bfloat16 [16384, 1024], P('blk', 'exp')
The draws below stay inside these ranges and needn't reach their ends.
Inputs may be any that keep to these rules, and one draw needn't show every extreme that they name: `positions`: a permutation of all positions of the stream. `segment_ids`: the document number never falls along the position in the stream, and every document holds a token. `cache_slots`: within each block of 1024 rows a permutation of 0 to 1023.
All inputs are finite; a program needn't handle non-finite values.
Results may differ from the reference program's by a relative error of at most 0.015.
Values may be sent and summed in bfloat16 or wider, within the bound.
No kernel may reach another device: no remote copies, remote signals or barrier semaphores. Data moves between devices by JAX's collectives and lax.ppermute only.
A program may use at most 128 MiB of HBM per device.

```python
import math
import jax
import jax.numpy as jnp
import numpy as np
from jax import lax

D = 2048
HD = 128
FE = 1408
TOP = 4
HEADS = 8
SHARED = 3072
NDOCS = 12
TOK_DEV = 128
TOKENS = 16384
GROUP = 1024
EXPERTS = 64
FH = 704
CAP = 10
DEVICES = 128


def stream_layout(key):
    base = jax.random.fold_in(key, 101)
    order = jax.random.permutation(jax.random.fold_in(base, 1), TOKENS).astype(jnp.int32)
    cuts = jax.random.permutation(jax.random.fold_in(base, 2), TOKENS - 1)[:NDOCS - 1].astype(jnp.int32) + 1
    spots = jnp.arange(TOKENS, dtype=jnp.int32)
    document = jnp.sum((spots[:, None] >= cuts[None, :]).astype(jnp.int32), axis=1).astype(jnp.int32)
    return (order, document[order])


def draw_positions(key, part):
    return stream_layout(key)[0]


def draw_segment_ids(key, part):
    return stream_layout(key)[1]


def draw_cache_slots(key, part):
    several = jax.random.split(jax.random.fold_in(key, 202), TOKENS // GROUP)
    tables = jax.vmap(lambda single: jax.random.permutation(single, GROUP))(several)
    return tables.reshape(-1).astype(jnp.int32)


def attention_pair(key):
    base = jax.random.fold_in(key, 303)
    width = HEADS * HD
    factor = D ** (-0.5)
    query = jax.random.normal(jax.random.fold_in(base, 1), (D, width), jnp.float32) * factor
    keyed = jax.random.normal(jax.random.fold_in(base, 2), (D, width), jnp.float32) * factor
    return (query, keyed)


def draw_query_weight(key, part):
    return attention_pair(key)[0].astype(jnp.bfloat16)


def draw_key_weight(key, part):
    return attention_pair(key)[1].astype(jnp.bfloat16)


def levels(stream_key, shape, shards, low, largest):
    loudness = 1.0
    for position, parts in shards:
        heights = jax.random.uniform(jax.random.fold_in(jax.random.fold_in(stream_key, 6), position), (parts,), jnp.float32, low / len(shards), largest / len(shards))
        loudness = loudness * jnp.repeat(jnp.exp(heights), shape[position] // parts).reshape((-1,) + (1,) * (len(shape) - 1 - position))
    return loudness


def shared_out(key, own, number, rows, number_of, top, bound, skew):
    sequence = jax.random.permutation(key, number_of)
    heavy_load, common = shares(number_of, rows * top, bound, skew, True), shares(number_of, rows * top, bound, skew, False)
    places = jnp.arange(number_of)

    def named(tallies, turn):
        used = int((tallies > 0).sum())
        fixed = max(1, used // 4)
        passed = fixed + (places - fixed + turn * (used - fixed)) % max(1, number_of - fixed)
        return jnp.zeros((number_of,), jnp.int32).at[sequence[jnp.where(places < fixed, places, passed)]].set(jnp.asarray(tallies, jnp.int32))

    tallies = jnp.where(number % 4 == 0, named(heavy_load, number // 4), named(common, number - number // 4 - 1))
    mixed = jax.random.permutation(jax.random.fold_in(own, 3), number_of)
    donor, sink = mixed[0:number_of // 2 * 2:2], mixed[1:number_of // 2 * 2:2]
    slack = jnp.minimum(tallies[donor] - 1, bound - tallies[sink]) // 2
    slack = jnp.where((donor == sequence[0]) | (sink == sequence[0]) | (tallies[sink] == 0), 0, jnp.maximum(slack, 0))
    passed = jax.random.randint(jax.random.fold_in(own, 4), (number_of // 2,), 0, 1 << 20) % (slack + 1)
    tallies = tallies.at[donor].add(-passed).at[sink].add(passed)
    items = jnp.searchsorted(jnp.cumsum(tallies), jnp.arange(rows * top), side="right").astype(jnp.int32)
    grid = items.reshape(top, rows).T
    grid = grid[jax.random.permutation(jax.random.fold_in(own, 1), rows)]
    turn = jax.random.randint(jax.random.fold_in(own, 2), (rows, 1), 0, top)
    return jnp.take_along_axis(grid, (jnp.arange(top)[None, :] + turn) % top, axis=1)


def shares(count, total, bound, lean, full):
    portions = [(1 << 20) // math.isqrt(standing ** lean) + 1 for standing in range(1, count + 1)]
    largest = bound if full else min(bound, max(-(-total // count), total * portions[0] // sum(portions)))
    least = 1 if total - largest >= count - 1 else 0
    holding, surplus = [largest] + [least] * (count - 1), total - largest - least * (count - 1)
    while surplus > 0:
        candidates = [i for i in range(1, count) if holding[i] < largest] or [i for i in range(1, count) if holding[i] < bound]
        mass, left = sum([portions[i] for i in candidates]), surplus
        for i in candidates:
            more = min(bound - holding[i], max(1, left * portions[i] // mass), surplus)
            holding[i] = holding[i] + more
            surplus = surplus - more
    return np.array(holding)


def scatter_about(own_key, dims, scale, limit, pieces=(), kind=jnp.bfloat16):
    level = levels(own_key, dims, pieces, -0.22, 0.18) if pieces else 1.0
    array = jax.random.normal(own_key, dims, jnp.float32) * scale * level
    return jnp.minimum(jnp.maximum(array, -limit), limit).astype(kind)


def setup_inputs(seed: int = 0) -> dict:
    arg_keys = jax.random.split(jax.random.key(seed), 20)
    stream = scatter_about(arg_keys[0], (TOKENS, D), 1.0, 6.0, ((0, 128),))
    norm_gain = jnp.clip(1.0 + 0.1 * jax.random.normal(arg_keys[1], (D,), jnp.float32), 0.5, 1.5)
    query_weight = draw_query_weight(jax.random.fold_in(arg_keys[19], 71), 0)
    key_weight = draw_key_weight(jax.random.fold_in(arg_keys[19], 71), 0)
    value_weight = scatter_about(arg_keys[4], (D, HEADS * HD), D ** -0.5, 0.125, ((1, 8),))
    output_weight = scatter_about(arg_keys[5], (HEADS * HD, D), (HEADS * HD) ** -0.5, 0.1875)
    post_gain = jnp.clip(1.0 + 0.1 * jax.random.normal(arg_keys[6], (D,), jnp.float32), 0.5, 1.5)
    shared_gate = scatter_about(arg_keys[7], (D, SHARED), D ** -0.5, 0.125, ((1, 8),))
    shared_up = scatter_about(arg_keys[8], (D, SHARED), D ** -0.5, 0.125, ((1, 8),))
    shared_down = scatter_about(arg_keys[9], (SHARED, D), SHARED ** -0.5, 0.109375, ((0, 8),))
    shared_router = scatter_about(arg_keys[10], (D,), D ** -0.5, 0.125)
    expert_gate = scatter_about(arg_keys[11], (2 * EXPERTS, D, FH), D ** -0.5, 0.125, ((0, 128),))
    expert_up = scatter_about(arg_keys[12], (2 * EXPERTS, D, FH), D ** -0.5, 0.125, ((0, 128),))
    expert_down = scatter_about(arg_keys[13], (2 * EXPERTS, FH, D), FE ** -0.5, 0.15625, ((0, 128),))
    expert_ids_keys = jax.random.split(jax.random.fold_in(arg_keys[14], 1), TOKENS // TOK_DEV)
    expert_ids_turns = jax.random.permutation(jax.random.fold_in(arg_keys[14], 3), TOKENS // TOK_DEV)
    expert_ids = jax.vmap(lambda own, number: shared_out(jax.random.fold_in(arg_keys[14], 2), own, number, TOK_DEV, EXPERTS, TOP, CAP, 2))(expert_ids_keys, expert_ids_turns).reshape((TOKENS, TOP))
    route_weights = jnp.clip(jnp.exp(math.log(0.5) - 2.3025851 * jax.random.uniform(arg_keys[15], (TOKENS, TOP), jnp.float32) ** levels(arg_keys[15], (TOKENS, TOP), ((0, 128),), -0.2, 0.2)), 0.05, 0.5)
    positions = draw_positions(jax.random.fold_in(arg_keys[19], 71), 0)
    segment_ids = draw_segment_ids(jax.random.fold_in(arg_keys[19], 71), 0)
    cache_slots = draw_cache_slots(jax.random.fold_in(arg_keys[19], 71), 0)
    return {"stream": stream, "norm_gain": norm_gain, "query_weight": query_weight, "key_weight": key_weight, "value_weight": value_weight, "output_weight": output_weight, "post_gain": post_gain, "shared_gate": shared_gate, "shared_up": shared_up, "shared_down": shared_down, "shared_router": shared_router, "expert_gate": expert_gate, "expert_up": expert_up, "expert_down": expert_down, "expert_ids": expert_ids, "route_weights": route_weights, "positions": positions, "segment_ids": segment_ids, "cache_slots": cache_slots}


EPS = 1e-06

def dot_float(left, right):
    return jnp.dot(left.astype(jnp.float32), right.astype(jnp.float32), preferred_element_type=jnp.float32)

def rms_norm(rows, gain):
    wide = rows.astype(jnp.float32)
    factor = lax.rsqrt(lax.optimization_barrier(jnp.mean(wide * wide, axis=-1, keepdims=True)) + EPS)
    return (wide * factor * gain).astype(jnp.bfloat16)

def attend_block(query_block, query_position, query_segment, head_keys, head_values):
    scores = dot_float(query_block, head_keys[0].T) * HD ** (-0.5)
    allowed = (head_keys[2][None, :] == query_segment[:, None]) & (head_keys[1][None, :] <= query_position[:, None])
    scores = jnp.where(allowed, scores, -1e+30)
    highest = lax.optimization_barrier(jnp.max(scores, axis=1, keepdims=True))
    probs = jnp.where(allowed, jnp.exp(scores - highest), 0.0)
    denom = lax.optimization_barrier(jnp.sum(probs, axis=1, keepdims=True))
    mixed = dot_float(probs.astype(jnp.bfloat16), head_values)
    return (mixed / denom).astype(jnp.bfloat16)

def reference(stream, norm_gain, query_weight, key_weight, value_weight, output_weight, post_gain, shared_gate, shared_up, shared_down, shared_router, expert_gate, expert_up, expert_down, expert_ids, route_weights, positions, segment_ids, cache_slots):
    normed = rms_norm(stream, norm_gain)
    queries = dot_float(normed, query_weight).astype(jnp.bfloat16)
    keys = dot_float(normed, key_weight).astype(jnp.bfloat16)
    values = dot_float(normed, value_weight).astype(jnp.bfloat16)
    block_total = TOKENS // GROUP

    def per_head(head):
        head_q = lax.dynamic_slice_in_dim(queries, head * HD, HD, 1)
        head_k = lax.dynamic_slice_in_dim(keys, head * HD, HD, 1)
        head_v = lax.dynamic_slice_in_dim(values, head * HD, HD, 1)

        def per_block(index):
            begin = index * GROUP
            query_block = lax.dynamic_slice_in_dim(head_q, begin, GROUP, 0)
            query_position = lax.dynamic_slice_in_dim(positions, begin, GROUP, 0)
            query_segment = lax.dynamic_slice_in_dim(segment_ids, begin, GROUP, 0)
            return attend_block(query_block, query_position, query_segment, (head_k, positions, segment_ids), head_v)
        return lax.map(per_block, jnp.arange(block_total, dtype=jnp.int32)).reshape(TOKENS, HD)
    heads_out = lax.map(per_head, jnp.arange(HEADS, dtype=jnp.int32))
    heads_out = jnp.transpose(heads_out, (1, 0, 2)).reshape(TOKENS, HEADS * HD)
    attended = dot_float(heads_out, output_weight)
    resid = (stream.astype(jnp.float32) + attended).astype(jnp.bfloat16)
    normed2 = rms_norm(resid, post_gain)
    shared_hidden = (jax.nn.silu(dot_float(normed2, shared_gate)) * dot_float(normed2, shared_up)).astype(jnp.bfloat16)
    shared = dot_float(shared_hidden, shared_down) * jax.nn.sigmoid(dot_float(normed2, shared_router[:, None]))
    pairs = expert_ids.reshape(DEVICES, TOK_DEV * TOP).astype(jnp.int32)
    onehot = (pairs[:, :, None] == jnp.arange(EXPERTS, dtype=jnp.int32)[None, None, :]).astype(jnp.int32)
    slots = lax.optimization_barrier(jnp.sum(onehot * (jnp.cumsum(onehot, axis=1) - 1), axis=2)).astype(jnp.int32)
    token_of = (jnp.arange(TOKENS, dtype=jnp.int32)[:, None] + jnp.zeros((1, TOP), jnp.int32)).reshape(DEVICES, TOK_DEV * TOP)
    holder = jnp.zeros_like(pairs) + jnp.arange(DEVICES, dtype=jnp.int32)[:, None]
    table = jnp.full((EXPERTS, DEVICES, CAP), TOKENS, jnp.int32).at[pairs, holder, slots].set(token_of)
    scales = jnp.zeros((EXPERTS, DEVICES, CAP), jnp.float32).at[pairs, holder, slots].set(route_weights.reshape(DEVICES, TOK_DEV * TOP).astype(jnp.float32))
    padded = jnp.concatenate([normed2, jnp.zeros((1, D), jnp.bfloat16)], axis=0)

    def serve(running, half):
        expert = half // 2
        row_index = table[expert].reshape(-1)
        row_scale = scales[expert].reshape(-1)
        chosen = padded[row_index]
        hidden = (jax.nn.silu(dot_float(chosen, expert_gate[half])) * dot_float(chosen, expert_up[half])).astype(jnp.bfloat16)
        result = lax.optimization_barrier(dot_float(hidden, expert_down[half]).astype(jnp.bfloat16)).astype(jnp.float32)
        return (running.at[row_index].add(row_scale[:, None] * result), None)
    routed, _ = lax.scan(serve, jnp.zeros((TOKENS + 1, D), jnp.float32), jnp.arange(2 * EXPERTS, dtype=jnp.int32))
    final = (resid.astype(jnp.float32) + shared + routed[:TOKENS]).astype(jnp.bfloat16)
    rows_at = jnp.arange(TOKENS, dtype=jnp.int32) // GROUP * GROUP + cache_slots.astype(jnp.int32)
    cache_keys = jnp.zeros((TOKENS, HEADS * HD), jnp.bfloat16).at[rows_at].set(keys)
    cache_values = jnp.zeros((TOKENS, HEADS * HD), jnp.bfloat16).at[rows_at].set(values)
    return (final, cache_keys, cache_values)
```

```python
import math

import jax
import jax.numpy as jnp
from jax import lax
from jax.sharding import PartitionSpec as P

D = 2048
HD = 128
TOP = 4


EPS = 1e-06
FLOOR_SCORE = -1e30


def rms_norm(rows, gain):
    wide = rows.astype(jnp.float32)
    factor = lax.rsqrt(jnp.mean(wide * wide, axis=-1, keepdims=True) + EPS)
    return (wide * factor * gain).astype(jnp.bfloat16)


def per_device(
    stream,
    norm_gain,
    query_weight,
    key_weight,
    value_weight,
    output_weight,
    post_gain,
    shared_gate,
    shared_up,
    shared_down,
    shared_router,
    expert_gate,
    expert_up,
    expert_down,
    expert_ids,
    route_weights,
    positions,
    segment_ids,
    cache_slots,
):
    local_rows = stream.shape[0]
    n_exp = lax.axis_size("exp")
    meta = jnp.stack([positions, segment_ids, cache_slots]).astype(jnp.float32)
    meta_all = lax.all_gather(meta, ("blk", "exp"), axis=0)
    all_position = meta_all[:, 0, :].reshape(-1).astype(jnp.int32)
    all_segment = meta_all[:, 1, :].reshape(-1).astype(jnp.int32)
    meta_group = lax.dynamic_slice_in_dim(meta_all, lax.axis_index("blk") * n_exp, n_exp, 0)
    group_position = meta_group[:, 0, :].reshape(-1).astype(jnp.int32)
    group_segment = meta_group[:, 1, :].reshape(-1).astype(jnp.int32)
    group_slot = meta_group[:, 2, :].reshape(-1).astype(jnp.int32)
    group_stream = lax.all_gather(stream, "exp", axis=0, tiled=True)
    group_size = group_stream.shape[0]
    normed = rms_norm(group_stream, norm_gain)
    queries = jnp.dot(normed, query_weight, preferred_element_type=jnp.float32).astype(jnp.bfloat16)
    keys = jnp.dot(normed, key_weight, preferred_element_type=jnp.float32).astype(jnp.bfloat16)
    values = jnp.dot(normed, value_weight, preferred_element_type=jnp.float32).astype(jnp.bfloat16)
    width = queries.shape[1]
    local_heads = width // HD
    cache_keys = jnp.zeros((group_size, width), jnp.bfloat16).at[group_slot].set(keys)
    cache_values = jnp.zeros((group_size, width), jnp.bfloat16).at[group_slot].set(values)
    query_heads = queries.reshape(group_size, local_heads, HD)
    factor = HD ** (-0.5)

    def attend(carry, block):
        highest, denom, summed = carry
        block_keys, block_values, block_position, block_segment = block
        scores = (
            jnp.einsum("qhd,khd->hqk", query_heads, block_keys, preferred_element_type=jnp.float32)
            * factor
        )
        allowed = (
            (block_segment[None, :] == group_segment[:, None])
            & (block_position[None, :] <= group_position[:, None])
        )[None]
        scores = jnp.where(allowed, scores, FLOOR_SCORE)
        newest = jnp.maximum(highest, jnp.max(scores, axis=2))
        probs = jnp.where(allowed, jnp.exp(scores - newest[:, :, None]), 0.0)
        shrink = jnp.exp(highest - newest)
        denom = denom * shrink + jnp.sum(probs, axis=2)
        summed = summed * shrink[:, :, None] + jnp.einsum(
            "hqk,khd->hqd",
            probs.astype(jnp.bfloat16),
            block_values,
            preferred_element_type=jnp.float32,
        )
        return ((newest, denom, summed), None)

    initial = (
        jnp.full((local_heads, group_size), FLOOR_SCORE, jnp.float32),
        jnp.zeros((local_heads, group_size), jnp.float32),
        jnp.zeros((local_heads, group_size, HD), jnp.float32),
    )
    key_heads = keys.reshape(group_size, local_heads, HD)
    value_heads = values.reshape(group_size, local_heads, HD)
    carry = initial
    piece = (
        lax.all_gather(key_heads, "blk", axis=0, tiled=True),
        lax.all_gather(value_heads, "blk", axis=0, tiled=True),
        all_position,
        all_segment,
    )
    piece_rows = piece[0].shape[0]
    block = math.gcd(piece_rows, 1024)
    count = piece_rows // block
    blocks = tuple((member.reshape((count, block) + member.shape[1:]) for member in piece))
    carry, _ = lax.scan(attend, carry, blocks)
    highest, denom, summed = carry
    heads_out = (summed / denom[:, :, None]).astype(jnp.bfloat16)
    heads_out = jnp.transpose(heads_out, (1, 0, 2)).reshape(group_size, width)
    owner = lax.axis_index("exp")
    local_output = lax.dynamic_slice_in_dim(output_weight, owner * width, width, 0)
    attended = lax.psum(
        jnp.dot(heads_out, local_output, preferred_element_type=jnp.float32).astype(jnp.bfloat16),
        "exp",
    ).astype(jnp.float32)
    resid_group = (group_stream.astype(jnp.float32) + attended).astype(jnp.bfloat16)
    resid_local = lax.dynamic_slice_in_dim(resid_group, owner * local_rows, local_rows, 0)
    normed_group = rms_norm(resid_group, post_gain)
    normed_local = lax.dynamic_slice_in_dim(normed_group, owner * local_rows, local_rows, 0)
    hidden = (
        jax.nn.silu(jnp.dot(normed_group, shared_gate, preferred_element_type=jnp.float32))
        * jnp.dot(normed_group, shared_up, preferred_element_type=jnp.float32)
    ).astype(jnp.bfloat16)
    opening = jax.nn.sigmoid(
        jnp.dot(normed_group, shared_router, preferred_element_type=jnp.float32)
    )
    shared_local = lax.psum_scatter(
        (
            jnp.dot(hidden, shared_down, preferred_element_type=jnp.float32) * opening[:, None]
        ).astype(jnp.bfloat16),
        "exp",
        scatter_dimension=0,
        tiled=True,
    ).astype(jnp.float32)
    experts = lax.axis_size(("blk", "exp")) // 2
    capacity = max(2, 5 * local_rows * TOP // (4 * experts))
    flat_ids = expert_ids.reshape(-1)
    onehot = (flat_ids[:, None] == jnp.arange(experts, dtype=jnp.int32)[None, :]).astype(jnp.int32)
    slots = jnp.sum(onehot * (jnp.cumsum(onehot, axis=0) - 1), axis=1)
    target = flat_ids * capacity + slots
    slot_ids = jnp.arange(experts * capacity, dtype=jnp.int32)
    pick = jnp.any(
        (target[None, :] == slot_ids[:, None]).reshape(experts * capacity, local_rows, TOP), axis=2
    )
    pick = jnp.broadcast_to(
        pick.reshape(experts, 1, capacity, local_rows), (experts, 2, capacity, local_rows)
    ).reshape(2 * experts * capacity, local_rows)
    outgoing = (
        jnp.dot(pick.astype(jnp.bfloat16), normed_local, preferred_element_type=jnp.float32)
        .astype(jnp.bfloat16)
        .reshape(2 * experts, capacity, D)
    )
    arrived = lax.all_to_all(outgoing, ("blk", "exp"), split_axis=0, concat_axis=0, tiled=True)
    leading = arrived.shape[:-1]
    flat_rows = arrived.reshape(-1, D)
    hidden = (
        jax.nn.silu(jnp.dot(flat_rows, expert_gate[0], preferred_element_type=jnp.float32))
        * jnp.dot(flat_rows, expert_up[0], preferred_element_type=jnp.float32)
    ).astype(jnp.bfloat16)
    returned = lax.all_to_all(
        jnp.dot(hidden, expert_down[0], preferred_element_type=jnp.float32)
        .astype(jnp.bfloat16)
        .reshape(leading + (D,)),
        ("blk", "exp"),
        split_axis=0,
        concat_axis=0,
        tiled=True,
    )
    column = jnp.arange(2 * experts * capacity, dtype=jnp.int32)
    column_target = column // (2 * capacity) * capacity + column % capacity
    gather_pick = (target[:, None] == column_target[None, :]).astype(jnp.bfloat16)
    picked = jnp.dot(
        gather_pick, returned.reshape(-1, D), preferred_element_type=jnp.float32
    ) * route_weights.reshape(-1)[:, None]
    routed = jnp.sum(picked.reshape(local_rows, TOP, D), axis=1)
    final = (resid_local.astype(jnp.float32) + shared_local + routed).astype(jnp.bfloat16)
    return (final, cache_keys, cache_values)


def solution(mesh):
    in_specs = (
        P(("blk", "exp"), None),
        P(),
        P(None, "exp"),
        P(None, "exp"),
        P(None, "exp"),
        P(),
        P(),
        P(None, "exp"),
        P(None, "exp"),
        P("exp", None),
        P(),
        P(("blk", "exp"), None, None),
        P(("blk", "exp"), None, None),
        P(("blk", "exp"), None, None),
        P(("blk", "exp"), None),
        P(("blk", "exp"), None),
        P(("blk", "exp")),
        P(("blk", "exp")),
        P(("blk", "exp")),
    )
    out_specs = (P(("blk", "exp"), None), P("blk", "exp"), P("blk", "exp"))
    return jax.shard_map(
        per_device, mesh=mesh, in_specs=in_specs, out_specs=out_specs, check_vma=False
    )
```

```python
import math

import jax
import jax.numpy as jnp
from jax import lax
from jax.sharding import Mesh, PartitionSpec as P

D = 2048
HD = 128
TOP = 4


EPS = 1e-06
FLOOR_SCORE = -1e30
EXP = ("x", "core")
CHIPS = ("blk", "x")


def rms_norm(rows, gain):
    wide = rows.astype(jnp.float32)
    factor = lax.rsqrt(jnp.mean(wide * wide, axis=-1, keepdims=True) + EPS)
    return (wide * factor * gain).astype(jnp.bfloat16)


def per_device(
    stream,
    norm_gain,
    query_weight,
    key_weight,
    value_weight,
    output_weight,
    post_gain,
    shared_gate,
    shared_up,
    shared_down,
    shared_router,
    expert_gate,
    expert_up,
    expert_down,
    expert_ids,
    route_weights,
    positions,
    segment_ids,
    cache_slots,
):
    local_rows = stream.shape[0]
    n_exp = lax.axis_size(EXP)
    meta = jnp.stack([positions, segment_ids, cache_slots]).astype(jnp.float32)
    meta_all = lax.all_gather(meta, ("blk",) + EXP, axis=0)
    all_position = meta_all[:, 0, :].reshape(-1).astype(jnp.int32)
    all_segment = meta_all[:, 1, :].reshape(-1).astype(jnp.int32)
    meta_group = lax.dynamic_slice_in_dim(meta_all, lax.axis_index("blk") * n_exp, n_exp, 0)
    group_position = meta_group[:, 0, :].reshape(-1).astype(jnp.int32)
    group_segment = meta_group[:, 1, :].reshape(-1).astype(jnp.int32)
    group_slot = meta_group[:, 2, :].reshape(-1).astype(jnp.int32)
    group_stream = lax.all_gather(stream, EXP, axis=0, tiled=True)
    group_size = group_stream.shape[0]
    normed = rms_norm(group_stream, norm_gain)
    queries = jnp.dot(normed, query_weight, preferred_element_type=jnp.float32).astype(jnp.bfloat16)
    keys = jnp.dot(normed, key_weight, preferred_element_type=jnp.float32).astype(jnp.bfloat16)
    values = jnp.dot(normed, value_weight, preferred_element_type=jnp.float32).astype(jnp.bfloat16)
    width = queries.shape[1]
    local_heads = width // HD
    cache_keys = jnp.zeros((group_size, width), jnp.bfloat16).at[group_slot].set(keys)
    cache_values = jnp.zeros((group_size, width), jnp.bfloat16).at[group_slot].set(values)
    query_heads = queries.reshape(group_size, local_heads, HD)
    factor = HD ** (-0.5)

    def attend(carry, block):
        highest, denom, summed = carry
        block_keys, block_values, block_position, block_segment = block
        scores = (
            jnp.einsum("qhd,khd->hqk", query_heads, block_keys, preferred_element_type=jnp.float32)
            * factor
        )
        allowed = (
            (block_segment[None, :] == group_segment[:, None])
            & (block_position[None, :] <= group_position[:, None])
        )[None]
        scores = jnp.where(allowed, scores, FLOOR_SCORE)
        newest = jnp.maximum(highest, jnp.max(scores, axis=2))
        probs = jnp.where(allowed, jnp.exp(scores - newest[:, :, None]), 0.0)
        shrink = jnp.exp(highest - newest)
        denom = denom * shrink + jnp.sum(probs, axis=2)
        summed = summed * shrink[:, :, None] + jnp.einsum(
            "hqk,khd->hqd",
            probs.astype(jnp.bfloat16),
            block_values,
            preferred_element_type=jnp.float32,
        )
        return ((newest, denom, summed), None)

    initial = (
        jnp.full((local_heads, group_size), FLOOR_SCORE, jnp.float32),
        jnp.zeros((local_heads, group_size), jnp.float32),
        jnp.zeros((local_heads, group_size, HD), jnp.float32),
    )
    key_heads = keys.reshape(group_size, local_heads, HD)
    value_heads = values.reshape(group_size, local_heads, HD)
    carry = initial
    piece = (
        lax.all_gather(key_heads, "blk", axis=0, tiled=True),
        lax.all_gather(value_heads, "blk", axis=0, tiled=True),
        all_position,
        all_segment,
    )
    piece_rows = piece[0].shape[0]
    block = math.gcd(piece_rows, 1024)
    count = piece_rows // block
    blocks = tuple((member.reshape((count, block) + member.shape[1:]) for member in piece))
    carry, _ = lax.scan(attend, carry, blocks)
    highest, denom, summed = carry
    heads_out = (summed / denom[:, :, None]).astype(jnp.bfloat16)
    heads_out = jnp.transpose(heads_out, (1, 0, 2)).reshape(group_size, width)
    heads_local = lax.all_to_all(heads_out, EXP, split_axis=0, concat_axis=0, tiled=True)
    heads_local = jnp.transpose(
        heads_local.reshape(n_exp, local_rows, width), (1, 0, 2)
    ).reshape(local_rows, n_exp * width)
    attended = jnp.dot(heads_local, output_weight, preferred_element_type=jnp.float32)
    resid_local = (stream.astype(jnp.float32) + attended).astype(jnp.bfloat16)
    normed_local = rms_norm(resid_local, post_gain)
    normed_group = lax.all_gather(normed_local, EXP, axis=0, tiled=True)
    hidden = (
        jax.nn.silu(jnp.dot(normed_group, shared_gate, preferred_element_type=jnp.float32))
        * jnp.dot(normed_group, shared_up, preferred_element_type=jnp.float32)
    ).astype(jnp.bfloat16)
    opening = jax.nn.sigmoid(
        jnp.dot(normed_group, shared_router, preferred_element_type=jnp.float32)
    )
    shared_local = lax.psum_scatter(
        (
            jnp.dot(hidden, shared_down, preferred_element_type=jnp.float32) * opening[:, None]
        ).astype(jnp.bfloat16),
        EXP,
        scatter_dimension=0,
        tiled=True,
    ).astype(jnp.float32)
    experts = lax.axis_size(CHIPS)
    capacity = max(2, 5 * local_rows * TOP // (4 * experts))
    flat_ids = expert_ids.reshape(-1)
    onehot = (flat_ids[:, None] == jnp.arange(experts, dtype=jnp.int32)[None, :]).astype(jnp.int32)
    slots = jnp.sum(onehot * (jnp.cumsum(onehot, axis=0) - 1), axis=1)
    target = flat_ids * capacity + slots
    slot_ids = jnp.arange(experts * capacity, dtype=jnp.int32)
    pick = jnp.any(
        (target[None, :] == slot_ids[:, None]).reshape(experts * capacity, local_rows, TOP), axis=2
    )
    outgoing = (
        jnp.dot(pick.astype(jnp.bfloat16), normed_local, preferred_element_type=jnp.float32)
        .astype(jnp.bfloat16)
        .reshape(experts, capacity, D)
    )
    arrived = lax.all_to_all(outgoing, CHIPS, split_axis=0, concat_axis=0, tiled=True)
    arrived = lax.all_gather(arrived, "core", axis=0)
    leading = arrived.shape[:-1]
    flat_rows = arrived.reshape(-1, D)
    hidden = (
        jax.nn.silu(jnp.dot(flat_rows, expert_gate[0], preferred_element_type=jnp.float32))
        * jnp.dot(flat_rows, expert_up[0], preferred_element_type=jnp.float32)
    ).astype(jnp.bfloat16)
    half_out = (
        jnp.dot(hidden, expert_down[0], preferred_element_type=jnp.float32)
        .astype(jnp.bfloat16)
        .reshape(leading + (D,))
    )
    both_halves = lax.all_to_all(half_out, "core", split_axis=0, concat_axis=0, tiled=True)
    summed_halves = (
        both_halves[0].astype(jnp.float32) + both_halves[1].astype(jnp.float32)
    ).astype(jnp.bfloat16)
    returned = lax.all_to_all(summed_halves, CHIPS, split_axis=0, concat_axis=0, tiled=True)
    gather_pick = (target[:, None] == slot_ids[None, :]).astype(jnp.bfloat16)
    picked = jnp.dot(
        gather_pick, returned.reshape(-1, D), preferred_element_type=jnp.float32
    ) * route_weights.reshape(-1)[:, None]
    routed = jnp.sum(picked.reshape(local_rows, TOP, D), axis=1)
    routed = jnp.sum(picked.reshape(local_rows, TOP, D), axis=1)
    final = (resid_local.astype(jnp.float32) + shared_local + routed).astype(jnp.bfloat16)
    return (final, cache_keys, cache_values)


def solution(mesh):
    blk, exp = mesh.shape["blk"], mesh.shape["exp"]
    chip_mesh = Mesh(mesh.devices.reshape(blk, exp // 2, 2), ("blk", "x", "core"))
    rows = ("blk",) + EXP
    in_specs = (
        P(rows, None),
        P(),
        P(None, EXP),
        P(None, EXP),
        P(None, EXP),
        P(),
        P(),
        P(None, EXP),
        P(None, EXP),
        P(EXP, None),
        P(),
        P(rows, None, None),
        P(rows, None, None),
        P(rows, None, None),
        P(rows, None),
        P(rows, None),
        P(rows),
        P(rows),
        P(rows),
    )
    out_specs = (P(rows, None), P("blk", EXP), P("blk", EXP))
    return jax.shard_map(
        per_device, mesh=chip_mesh, in_specs=in_specs, out_specs=out_specs, check_vma=False
    )
```

```python
import math

import jax
import jax.numpy as jnp
from jax import lax
from jax.sharding import Mesh, PartitionSpec as P

D = 2048
HD = 128
TOP = 4


EPS = 1e-06
FLOOR_SCORE = -1e30
EXP = ("x", "core")
CHIPS = ("blk", "x")


def rms_norm(rows, gain):
    wide = rows.astype(jnp.float32)
    factor = lax.rsqrt(jnp.mean(wide * wide, axis=-1, keepdims=True) + EPS)
    return (wide * factor * gain).astype(jnp.bfloat16)


def per_device(
    stream,
    norm_gain,
    query_weight,
    key_weight,
    value_weight,
    output_weight,
    post_gain,
    shared_gate,
    shared_up,
    shared_down,
    shared_router,
    expert_gate,
    expert_up,
    expert_down,
    expert_ids,
    route_weights,
    positions,
    segment_ids,
    cache_slots,
):
    local_rows = stream.shape[0]
    n_exp = lax.axis_size(EXP)
    meta = jnp.stack([positions, segment_ids, cache_slots]).astype(jnp.float32)
    meta_all = lax.all_gather(meta, ("blk",) + EXP, axis=0)
    all_position = meta_all[:, 0, :].reshape(-1).astype(jnp.int32)
    all_segment = meta_all[:, 1, :].reshape(-1).astype(jnp.int32)
    meta_group = lax.dynamic_slice_in_dim(meta_all, lax.axis_index("blk") * n_exp, n_exp, 0)
    group_position = meta_group[:, 0, :].reshape(-1).astype(jnp.int32)
    group_segment = meta_group[:, 1, :].reshape(-1).astype(jnp.int32)
    group_slot = meta_group[:, 2, :].reshape(-1).astype(jnp.int32)
    group_stream = lax.all_gather(stream, EXP, axis=0, tiled=True)
    group_size = group_stream.shape[0]
    normed = rms_norm(group_stream, norm_gain)
    queries = jnp.dot(normed, query_weight, preferred_element_type=jnp.float32).astype(jnp.bfloat16)
    keys = jnp.dot(normed, key_weight, preferred_element_type=jnp.float32).astype(jnp.bfloat16)
    values = jnp.dot(normed, value_weight, preferred_element_type=jnp.float32).astype(jnp.bfloat16)
    width = queries.shape[1]
    local_heads = width // HD
    cache_keys = jnp.zeros((group_size, width), jnp.bfloat16).at[group_slot].set(keys)
    cache_values = jnp.zeros((group_size, width), jnp.bfloat16).at[group_slot].set(values)
    query_heads = queries.reshape(group_size, local_heads, HD)
    factor = HD ** (-0.5)

    def attend(carry, block):
        highest, denom, summed = carry
        block_keys, block_values, block_position, block_segment = block
        scores = (
            jnp.einsum("qhd,khd->hqk", query_heads, block_keys, preferred_element_type=jnp.float32)
            * factor
        )
        allowed = (
            (block_segment[None, :] == group_segment[:, None])
            & (block_position[None, :] <= group_position[:, None])
        )[None]
        scores = jnp.where(allowed, scores, FLOOR_SCORE)
        newest = jnp.maximum(highest, jnp.max(scores, axis=2))
        probs = jnp.where(allowed, jnp.exp(scores - newest[:, :, None]), 0.0)
        shrink = jnp.exp(highest - newest)
        denom = denom * shrink + jnp.sum(probs, axis=2)
        summed = summed * shrink[:, :, None] + jnp.einsum(
            "hqk,khd->hqd",
            probs.astype(jnp.bfloat16),
            block_values,
            preferred_element_type=jnp.float32,
        )
        return ((newest, denom, summed), None)

    initial = (
        jnp.full((local_heads, group_size), FLOOR_SCORE, jnp.float32),
        jnp.zeros((local_heads, group_size), jnp.float32),
        jnp.zeros((local_heads, group_size, HD), jnp.float32),
    )
    key_heads = keys.reshape(group_size, local_heads, HD)
    value_heads = values.reshape(group_size, local_heads, HD)
    carry = initial
    piece = (
        lax.all_gather(key_heads, "blk", axis=0, tiled=True),
        lax.all_gather(value_heads, "blk", axis=0, tiled=True),
        all_position,
        all_segment,
    )
    piece_rows = piece[0].shape[0]
    block = math.gcd(piece_rows, 1024)
    count = piece_rows // block
    blocks = tuple((member.reshape((count, block) + member.shape[1:]) for member in piece))
    carry, _ = lax.scan(attend, carry, blocks)
    highest, denom, summed = carry
    heads_out = (summed / denom[:, :, None]).astype(jnp.bfloat16)
    heads_out = jnp.transpose(heads_out, (1, 0, 2)).reshape(group_size, width)
    heads_local = lax.all_to_all(heads_out, EXP, split_axis=0, concat_axis=0, tiled=True)
    heads_local = jnp.transpose(
        heads_local.reshape(n_exp, local_rows, width), (1, 0, 2)
    ).reshape(local_rows, n_exp * width)
    attended = jnp.dot(heads_local, output_weight, preferred_element_type=jnp.float32)
    resid_local = (stream.astype(jnp.float32) + attended).astype(jnp.bfloat16)
    normed_local = rms_norm(resid_local, post_gain)
    normed_group = lax.all_gather(normed_local, EXP, axis=0, tiled=True)
    hidden = (
        jax.nn.silu(jnp.dot(normed_group, shared_gate, preferred_element_type=jnp.float32))
        * jnp.dot(normed_group, shared_up, preferred_element_type=jnp.float32)
    ).astype(jnp.bfloat16)
    opening = jax.nn.sigmoid(
        jnp.dot(normed_group, shared_router, preferred_element_type=jnp.float32)
    )
    shared_local = lax.psum_scatter(
        (
            jnp.dot(hidden, shared_down, preferred_element_type=jnp.float32) * opening[:, None]
        ).astype(jnp.bfloat16),
        EXP,
        scatter_dimension=0,
        tiled=True,
    ).astype(jnp.float32)
    experts = lax.axis_size(CHIPS)
    capacity = -(-max(2, 5 * local_rows * TOP // (4 * experts)) // 16) * 16
    flat_ids = expert_ids.reshape(-1)
    onehot = (flat_ids[:, None] == jnp.arange(experts, dtype=jnp.int32)[None, :]).astype(jnp.int32)
    slots = jnp.sum(onehot * (jnp.cumsum(onehot, axis=0) - 1), axis=1)
    target = flat_ids * capacity + slots
    slot_ids = jnp.arange(experts * capacity, dtype=jnp.int32)
    pick = jnp.any(
        (target[None, :] == slot_ids[:, None]).reshape(experts * capacity, local_rows, TOP), axis=2
    )
    outgoing = (
        jnp.dot(pick.astype(jnp.bfloat16), normed_local, preferred_element_type=jnp.float32)
        .astype(jnp.bfloat16)
        .reshape(experts, capacity, D)
    )
    arrived = lax.all_to_all(outgoing, CHIPS, split_axis=0, concat_axis=0, tiled=True)
    arrived = lax.all_gather(arrived, "core", axis=0)
    leading = arrived.shape[:-1]
    flat_rows = arrived.reshape(-1, D)
    hidden = (
        jax.nn.silu(jnp.dot(flat_rows, expert_gate[0], preferred_element_type=jnp.float32))
        * jnp.dot(flat_rows, expert_up[0], preferred_element_type=jnp.float32)
    ).astype(jnp.bfloat16)
    half_out = (
        jnp.dot(hidden, expert_down[0], preferred_element_type=jnp.float32)
        .astype(jnp.bfloat16)
        .reshape(leading + (D,))
    )
    both_halves = lax.all_to_all(half_out, "core", split_axis=0, concat_axis=0, tiled=True)
    summed_halves = (
        both_halves[0].astype(jnp.float32) + both_halves[1].astype(jnp.float32)
    ).astype(jnp.bfloat16)
    returned = lax.all_to_all(summed_halves, CHIPS, split_axis=0, concat_axis=0, tiled=True)
    gather_pick = (target[:, None] == slot_ids[None, :]).astype(jnp.bfloat16)
    picked = jnp.dot(
        gather_pick, returned.reshape(-1, D), preferred_element_type=jnp.float32
    ) * route_weights.reshape(-1)[:, None]
    routed = jnp.sum(picked.reshape(local_rows, TOP, D), axis=1)
    routed = jnp.sum(picked.reshape(local_rows, TOP, D), axis=1)
    final = (resid_local.astype(jnp.float32) + shared_local + routed).astype(jnp.bfloat16)
    return (final, cache_keys, cache_values)


def solution(mesh):
    blk, exp = mesh.shape["blk"], mesh.shape["exp"]
    chip_mesh = Mesh(mesh.devices.reshape(blk, exp // 2, 2), ("blk", "x", "core"))
    rows = ("blk",) + EXP
    in_specs = (
        P(rows, None),
        P(),
        P(None, EXP),
        P(None, EXP),
        P(None, EXP),
        P(),
        P(),
        P(None, EXP),
        P(None, EXP),
        P(EXP, None),
        P(),
        P(rows, None, None),
        P(rows, None, None),
        P(rows, None, None),
        P(rows, None),
        P(rows, None),
        P(rows),
        P(rows),
        P(rows),
    )
    out_specs = (P(rows, None), P("blk", EXP), P("blk", EXP))
    return jax.shard_map(
        per_device, mesh=chip_mesh, in_specs=in_specs, out_specs=out_specs, check_vma=False
    )
```

```python
import math

import jax
import jax.numpy as jnp
from jax import lax
from jax.sharding import Mesh, PartitionSpec as P

D = 2048
HD = 128
TOP = 4


EPS = 1e-06
FLOOR_SCORE = -1e30
EXP = ("x", "core")
CHIPS = ("blk", "x")


def rms_norm(rows, gain):
    wide = rows.astype(jnp.float32)
    factor = lax.rsqrt(jnp.mean(wide * wide, axis=-1, keepdims=True) + EPS)
    return (wide * factor * gain).astype(jnp.bfloat16)


def per_device(
    stream,
    norm_gain,
    query_weight,
    key_weight,
    value_weight,
    output_weight,
    post_gain,
    shared_gate,
    shared_up,
    shared_down,
    shared_router,
    expert_gate,
    expert_up,
    expert_down,
    expert_ids,
    route_weights,
    positions,
    segment_ids,
    cache_slots,
):
    local_rows = stream.shape[0]
    n_exp = lax.axis_size(EXP)
    meta = jnp.stack([positions, segment_ids, cache_slots]).astype(jnp.int32)
    meta_group = lax.all_gather(meta, EXP, axis=0)
    group_position = meta_group[:, 0, :].reshape(-1)
    group_segment = meta_group[:, 1, :].reshape(-1)
    group_slot = meta_group[:, 2, :].reshape(-1)
    group_stream = lax.all_gather(stream, EXP, axis=0, tiled=True)
    group_size = group_stream.shape[0]
    normed = rms_norm(group_stream, norm_gain)
    queries = jnp.dot(normed, query_weight, preferred_element_type=jnp.float32).astype(jnp.bfloat16)
    keys = jnp.dot(normed, key_weight, preferred_element_type=jnp.float32).astype(jnp.bfloat16)
    values = jnp.dot(normed, value_weight, preferred_element_type=jnp.float32).astype(jnp.bfloat16)
    width = queries.shape[1]
    local_heads = width // HD
    cache_keys = jnp.zeros((group_size, width), jnp.bfloat16).at[group_slot].set(keys)
    cache_values = jnp.zeros((group_size, width), jnp.bfloat16).at[group_slot].set(values)
    query_heads = queries.reshape(group_size, local_heads, HD)
    factor = HD ** (-0.5)

    def attend(carry, block):
        highest, denom, summed = carry
        block_keys, block_values, block_position, block_segment = block
        scores = (
            jnp.einsum("qhd,khd->hqk", query_heads, block_keys, preferred_element_type=jnp.float32)
            * factor
        )
        allowed = (
            (block_segment[None, :] == group_segment[:, None])
            & (block_position[None, :] <= group_position[:, None])
        )[None]
        scores = jnp.where(allowed, scores, FLOOR_SCORE)
        newest = jnp.maximum(highest, jnp.max(scores, axis=2))
        probs = jnp.where(allowed, jnp.exp(scores - newest[:, :, None]), 0.0)
        shrink = jnp.exp(highest - newest)
        denom = denom * shrink + jnp.sum(probs, axis=2)
        summed = summed * shrink[:, :, None] + jnp.einsum(
            "hqk,khd->hqd",
            probs.astype(jnp.bfloat16),
            block_values,
            preferred_element_type=jnp.float32,
        )
        return ((newest, denom, summed), None)

    initial = (
        jnp.full((local_heads, group_size), FLOOR_SCORE, jnp.float32),
        jnp.zeros((local_heads, group_size), jnp.float32),
        jnp.zeros((local_heads, group_size, HD), jnp.float32),
    )
    key_heads = keys.reshape(group_size, local_heads, HD)
    value_heads = values.reshape(group_size, local_heads, HD)
    n_blk = lax.axis_size("blk")
    ring = [(i, (i + 1) % n_blk) for i in range(n_blk)]

    def ring_step(state, _):
        carry, block = state
        carry, _ = attend(carry, block)
        block = lax.ppermute(block, "blk", ring)
        return ((carry, block), None)

    block = (key_heads, value_heads, group_position, group_segment)
    (carry, block), _ = lax.scan(ring_step, (initial, block), None, length=n_blk - 1)
    carry, _ = attend(carry, block)
    highest, denom, summed = carry
    heads_out = (summed / denom[:, :, None]).astype(jnp.bfloat16)
    heads_out = jnp.transpose(heads_out, (1, 0, 2)).reshape(group_size, width)
    heads_local = lax.all_to_all(heads_out, EXP, split_axis=0, concat_axis=0, tiled=True)
    heads_local = jnp.transpose(
        heads_local.reshape(n_exp, local_rows, width), (1, 0, 2)
    ).reshape(local_rows, n_exp * width)
    attended = jnp.dot(heads_local, output_weight, preferred_element_type=jnp.float32)
    resid_local = (stream.astype(jnp.float32) + attended).astype(jnp.bfloat16)
    normed_local = rms_norm(resid_local, post_gain)
    normed_group = lax.all_gather(normed_local, EXP, axis=0, tiled=True)
    hidden = (
        jax.nn.silu(jnp.dot(normed_group, shared_gate, preferred_element_type=jnp.float32))
        * jnp.dot(normed_group, shared_up, preferred_element_type=jnp.float32)
    ).astype(jnp.bfloat16)
    opening = jax.nn.sigmoid(
        jnp.dot(normed_group, shared_router, preferred_element_type=jnp.float32)
    )
    shared_local = lax.psum_scatter(
        (
            jnp.dot(hidden, shared_down, preferred_element_type=jnp.float32) * opening[:, None]
        ).astype(jnp.bfloat16),
        EXP,
        scatter_dimension=0,
        tiled=True,
    ).astype(jnp.float32)
    experts = lax.axis_size(CHIPS)
    capacity = -(-max(2, 5 * local_rows * TOP // (4 * experts)) // 16) * 16
    flat_ids = expert_ids.reshape(-1)
    onehot = (flat_ids[:, None] == jnp.arange(experts, dtype=jnp.int32)[None, :]).astype(jnp.int32)
    slots = jnp.sum(onehot * (jnp.cumsum(onehot, axis=0) - 1), axis=1)
    target = flat_ids * capacity + slots
    slot_ids = jnp.arange(experts * capacity, dtype=jnp.int32)
    pick = jnp.any(
        (target[None, :] == slot_ids[:, None]).reshape(experts * capacity, local_rows, TOP), axis=2
    )
    outgoing = (
        jnp.dot(pick.astype(jnp.bfloat16), normed_local, preferred_element_type=jnp.float32)
        .astype(jnp.bfloat16)
        .reshape(experts, capacity, D)
    )
    arrived = lax.all_to_all(outgoing, CHIPS, split_axis=0, concat_axis=0, tiled=True)
    arrived = lax.all_gather(arrived, "core", axis=0)
    leading = arrived.shape[:-1]
    flat_rows = arrived.reshape(-1, D)
    hidden = (
        jax.nn.silu(jnp.dot(flat_rows, expert_gate[0], preferred_element_type=jnp.float32))
        * jnp.dot(flat_rows, expert_up[0], preferred_element_type=jnp.float32)
    ).astype(jnp.bfloat16)
    half_out = (
        jnp.dot(hidden, expert_down[0], preferred_element_type=jnp.float32)
        .astype(jnp.bfloat16)
        .reshape(leading + (D,))
    )
    both_halves = lax.all_to_all(half_out, "core", split_axis=0, concat_axis=0, tiled=True)
    summed_halves = (
        both_halves[0].astype(jnp.float32) + both_halves[1].astype(jnp.float32)
    ).astype(jnp.bfloat16)
    returned = lax.all_to_all(summed_halves, CHIPS, split_axis=0, concat_axis=0, tiled=True)
    gather_pick = (target[:, None] == slot_ids[None, :]).astype(jnp.bfloat16)
    picked = jnp.dot(
        gather_pick, returned.reshape(-1, D), preferred_element_type=jnp.float32
    ) * route_weights.reshape(-1)[:, None]
    routed = jnp.sum(picked.reshape(local_rows, TOP, D), axis=1)
    routed = jnp.sum(picked.reshape(local_rows, TOP, D), axis=1)
    final = (resid_local.astype(jnp.float32) + shared_local + routed).astype(jnp.bfloat16)
    return (final, cache_keys, cache_values)


def solution(mesh):
    blk, exp = mesh.shape["blk"], mesh.shape["exp"]
    chip_mesh = Mesh(mesh.devices.reshape(blk, exp // 2, 2), ("blk", "x", "core"))
    rows = ("blk",) + EXP
    in_specs = (
        P(rows, None),
        P(),
        P(None, EXP),
        P(None, EXP),
        P(None, EXP),
        P(),
        P(),
        P(None, EXP),
        P(None, EXP),
        P(EXP, None),
        P(),
        P(rows, None, None),
        P(rows, None, None),
        P(rows, None, None),
        P(rows, None),
        P(rows, None),
        P(rows),
        P(rows),
        P(rows),
    )
    out_specs = (P(rows, None), P("blk", EXP), P("blk", EXP))
    return jax.shard_map(
        per_device, mesh=chip_mesh, in_specs=in_specs, out_specs=out_specs, check_vma=False
    )
```

```python
import math

import jax
import jax.numpy as jnp
from jax import lax
from jax.sharding import Mesh, PartitionSpec as P

D = 2048
HD = 128
TOP = 4


EPS = 1e-06
FLOOR_SCORE = -1e30
EXP = ("x", "core")
CHIPS = ("blk", "x")


def rms_norm(rows, gain):
    wide = rows.astype(jnp.float32)
    factor = lax.rsqrt(jnp.mean(wide * wide, axis=-1, keepdims=True) + EPS)
    return (wide * factor * gain).astype(jnp.bfloat16)


def per_device(
    stream,
    norm_gain,
    query_weight,
    key_weight,
    value_weight,
    output_weight,
    post_gain,
    shared_gate,
    shared_up,
    shared_down,
    shared_router,
    expert_gate,
    expert_up,
    expert_down,
    expert_ids,
    route_weights,
    positions,
    segment_ids,
    cache_slots,
):
    local_rows = stream.shape[0]
    n_exp = lax.axis_size(EXP)
    meta = jnp.stack([positions, segment_ids, cache_slots]).astype(jnp.int32)
    group_position, group_segment, group_slot = lax.all_gather(meta, EXP, axis=1, tiled=True)
    group_stream = lax.all_gather(stream, EXP, axis=0, tiled=True)
    group_size = group_stream.shape[0]
    normed = rms_norm(group_stream, norm_gain)
    queries = jnp.dot(normed, query_weight, preferred_element_type=jnp.float32).astype(jnp.bfloat16)
    keys = jnp.dot(normed, key_weight, preferred_element_type=jnp.float32).astype(jnp.bfloat16)
    values = jnp.dot(normed, value_weight, preferred_element_type=jnp.float32).astype(jnp.bfloat16)
    width = queries.shape[1]
    local_heads = width // HD
    cache_keys = jnp.zeros((group_size, width), jnp.bfloat16).at[group_slot].set(keys)
    cache_values = jnp.zeros((group_size, width), jnp.bfloat16).at[group_slot].set(values)
    query_heads = queries.reshape(group_size, local_heads, HD)
    factor = HD ** (-0.5)

    def attend(carry, block):
        highest, denom, summed = carry
        block_keys, block_values, block_position, block_segment = block
        scores = (
            jnp.einsum("qhd,khd->hqk", query_heads, block_keys, preferred_element_type=jnp.float32)
            * factor
        )
        allowed = (
            (block_segment[None, :] == group_segment[:, None])
            & (block_position[None, :] <= group_position[:, None])
        )[None]
        scores = jnp.where(allowed, scores, FLOOR_SCORE)
        newest = jnp.maximum(highest, jnp.max(scores, axis=2))
        probs = jnp.where(allowed, jnp.exp(scores - newest[:, :, None]), 0.0)
        shrink = jnp.exp(highest - newest)
        denom = denom * shrink + jnp.sum(probs, axis=2)
        summed = summed * shrink[:, :, None] + jnp.einsum(
            "hqk,khd->hqd",
            probs.astype(jnp.bfloat16),
            block_values,
            preferred_element_type=jnp.float32,
        )
        return ((newest, denom, summed), None)

    initial = (
        jnp.full((local_heads, group_size), FLOOR_SCORE, jnp.float32),
        jnp.zeros((local_heads, group_size), jnp.float32),
        jnp.zeros((local_heads, group_size, HD), jnp.float32),
    )
    key_heads = keys.reshape(group_size, local_heads, HD)
    value_heads = values.reshape(group_size, local_heads, HD)
    carry = initial
    coded = (
        jnp.stack([group_position // 128, group_position % 128, group_segment])
        .astype(jnp.bfloat16)
        .reshape(-1, width)
    )
    coded_rows = coded.shape[0]
    keys_coded = lax.all_gather(
        jnp.concatenate([keys, coded], axis=0), "blk", axis=0, tiled=True
    ).reshape(-1, group_size + coded_rows, width)
    coded_all = keys_coded[:, group_size:].reshape(-1, 3, group_size).astype(jnp.int32)
    piece = (
        keys_coded[:, :group_size].reshape(-1, local_heads, HD),
        lax.all_gather(value_heads, "blk", axis=0, tiled=True),
        (coded_all[:, 0] * 128 + coded_all[:, 1]).reshape(-1),
        coded_all[:, 2].reshape(-1),
    )
    piece_rows = piece[0].shape[0]
    block = math.gcd(piece_rows, 1024)
    count = piece_rows // block
    blocks = tuple((member.reshape((count, block) + member.shape[1:]) for member in piece))
    carry, _ = lax.scan(attend, carry, blocks)
    highest, denom, summed = carry
    heads_out = (summed / denom[:, :, None]).astype(jnp.bfloat16)
    heads_out = jnp.transpose(heads_out, (1, 0, 2)).reshape(group_size, width)
    heads_local = lax.all_to_all(heads_out, EXP, split_axis=0, concat_axis=0, tiled=True)
    heads_local = jnp.transpose(
        heads_local.reshape(n_exp, local_rows, width), (1, 0, 2)
    ).reshape(local_rows, n_exp * width)
    attended = jnp.dot(heads_local, output_weight, preferred_element_type=jnp.float32)
    resid_local = (stream.astype(jnp.float32) + attended).astype(jnp.bfloat16)
    normed_local = rms_norm(resid_local, post_gain)
    normed_group = lax.all_gather(normed_local, EXP, axis=0, tiled=True)
    hidden = (
        jax.nn.silu(jnp.dot(normed_group, shared_gate, preferred_element_type=jnp.float32))
        * jnp.dot(normed_group, shared_up, preferred_element_type=jnp.float32)
    ).astype(jnp.bfloat16)
    opening = jax.nn.sigmoid(
        jnp.dot(normed_group, shared_router, preferred_element_type=jnp.float32)
    )
    shared_local = lax.psum_scatter(
        (
            jnp.dot(hidden, shared_down, preferred_element_type=jnp.float32) * opening[:, None]
        ).astype(jnp.bfloat16),
        EXP,
        scatter_dimension=0,
        tiled=True,
    ).astype(jnp.float32)
    experts = lax.axis_size(CHIPS)
    capacity = -(-max(2, 5 * local_rows * TOP // (4 * experts)) // 16) * 16
    flat_ids = expert_ids.reshape(-1)
    onehot = (flat_ids[:, None] == jnp.arange(experts, dtype=jnp.int32)[None, :]).astype(jnp.int32)
    slots = jnp.sum(onehot * (jnp.cumsum(onehot, axis=0) - 1), axis=1)
    target = flat_ids * capacity + slots
    slot_ids = jnp.arange(experts * capacity, dtype=jnp.int32)
    pick = jnp.any(
        (target[None, :] == slot_ids[:, None]).reshape(experts * capacity, local_rows, TOP), axis=2
    )
    outgoing = (
        jnp.dot(pick.astype(jnp.bfloat16), normed_local, preferred_element_type=jnp.float32)
        .astype(jnp.bfloat16)
        .reshape(experts, capacity, D)
    )
    arrived = lax.all_to_all(outgoing, CHIPS, split_axis=0, concat_axis=0, tiled=True)
    arrived = lax.all_gather(arrived, "core", axis=0)
    leading = arrived.shape[:-1]
    flat_rows = arrived.reshape(-1, D)
    hidden = (
        jax.nn.silu(jnp.dot(flat_rows, expert_gate[0], preferred_element_type=jnp.float32))
        * jnp.dot(flat_rows, expert_up[0], preferred_element_type=jnp.float32)
    ).astype(jnp.bfloat16)
    half_out = (
        jnp.dot(hidden, expert_down[0], preferred_element_type=jnp.float32)
        .astype(jnp.bfloat16)
        .reshape(leading + (D,))
    )
    both_halves = lax.all_to_all(half_out, "core", split_axis=0, concat_axis=0, tiled=True)
    summed_halves = (
        both_halves[0].astype(jnp.float32) + both_halves[1].astype(jnp.float32)
    ).astype(jnp.bfloat16)
    returned = lax.all_to_all(summed_halves, CHIPS, split_axis=0, concat_axis=0, tiled=True)
    gather_pick = (target[:, None] == slot_ids[None, :]).astype(jnp.bfloat16)
    picked = jnp.dot(
        gather_pick, returned.reshape(-1, D), preferred_element_type=jnp.float32
    ) * route_weights.reshape(-1)[:, None]
    routed = jnp.sum(picked.reshape(local_rows, TOP, D), axis=1)
    routed = jnp.sum(picked.reshape(local_rows, TOP, D), axis=1)
    final = (resid_local.astype(jnp.float32) + shared_local + routed).astype(jnp.bfloat16)
    return (final, cache_keys, cache_values)


def solution(mesh):
    blk, exp = mesh.shape["blk"], mesh.shape["exp"]
    chip_mesh = Mesh(mesh.devices.reshape(blk, exp // 2, 2), ("blk", "x", "core"))
    rows = ("blk",) + EXP
    in_specs = (
        P(rows, None),
        P(),
        P(None, EXP),
        P(None, EXP),
        P(None, EXP),
        P(),
        P(),
        P(None, EXP),
        P(None, EXP),
        P(EXP, None),
        P(),
        P(rows, None, None),
        P(rows, None, None),
        P(rows, None, None),
        P(rows, None),
        P(rows, None),
        P(rows),
        P(rows),
        P(rows),
    )
    out_specs = (P(rows, None), P("blk", EXP), P("blk", EXP))
    return jax.shard_map(
        per_device, mesh=chip_mesh, in_specs=in_specs, out_specs=out_specs, check_vma=False
    )
```

```python
import math

import jax
import jax.numpy as jnp
from jax import lax
from jax.sharding import Mesh, PartitionSpec as P

D = 2048
HD = 128
TOP = 4


EPS = 1e-06
FLOOR_SCORE = -1e30
EXP = ("x", "core")
CHIPS = ("blk", "x")
RING = [None]


def rms_norm(rows, gain):
    wide = rows.astype(jnp.float32)
    factor = lax.rsqrt(jnp.mean(wide * wide, axis=-1, keepdims=True) + EPS)
    return (wide * factor * gain).astype(jnp.bfloat16)


def per_device(
    stream,
    norm_gain,
    query_weight,
    key_weight,
    value_weight,
    output_weight,
    post_gain,
    shared_gate,
    shared_up,
    shared_down,
    shared_router,
    expert_gate,
    expert_up,
    expert_down,
    expert_ids,
    route_weights,
    positions,
    segment_ids,
    cache_slots,
):
    local_rows = stream.shape[0]
    n_exp = lax.axis_size(EXP)
    meta = jnp.stack([positions, segment_ids, cache_slots]).astype(jnp.int32)
    group_position, group_segment, group_slot = lax.all_gather(meta, EXP, axis=1, tiled=True)
    group_stream = lax.all_gather(stream, EXP, axis=0, tiled=True)
    group_size = group_stream.shape[0]
    normed = rms_norm(group_stream, norm_gain)
    queries = jnp.dot(normed, query_weight, preferred_element_type=jnp.float32).astype(jnp.bfloat16)
    keys = jnp.dot(normed, key_weight, preferred_element_type=jnp.float32).astype(jnp.bfloat16)
    values = jnp.dot(normed, value_weight, preferred_element_type=jnp.float32).astype(jnp.bfloat16)
    width = queries.shape[1]
    local_heads = width // HD
    cache_keys = jnp.zeros((group_size, width), jnp.bfloat16).at[group_slot].set(keys)
    cache_values = jnp.zeros((group_size, width), jnp.bfloat16).at[group_slot].set(values)
    query_heads = queries.reshape(group_size, local_heads, HD)
    factor = HD ** (-0.5)

    def attend(carry, block):
        highest, denom, summed = carry
        block_keys, block_values, block_position, block_segment = block
        scores = (
            jnp.einsum("qhd,khd->hqk", query_heads, block_keys, preferred_element_type=jnp.float32)
            * factor
        )
        allowed = (
            (block_segment[None, :] == group_segment[:, None])
            & (block_position[None, :] <= group_position[:, None])
        )[None]
        scores = jnp.where(allowed, scores, FLOOR_SCORE)
        newest = jnp.maximum(highest, jnp.max(scores, axis=2))
        probs = jnp.where(allowed, jnp.exp(scores - newest[:, :, None]), 0.0)
        shrink = jnp.exp(highest - newest)
        denom = denom * shrink + jnp.sum(probs, axis=2)
        summed = summed * shrink[:, :, None] + jnp.einsum(
            "hqk,khd->hqd",
            probs.astype(jnp.bfloat16),
            block_values,
            preferred_element_type=jnp.float32,
        )
        return ((newest, denom, summed), None)

    initial = (
        jnp.full((local_heads, group_size), FLOOR_SCORE, jnp.float32),
        jnp.zeros((local_heads, group_size), jnp.float32),
        jnp.zeros((local_heads, group_size, HD), jnp.float32),
    )
    n_blk = lax.axis_size("blk")
    coded = (
        jnp.stack([group_position // 128, group_position % 128, group_segment])
        .astype(jnp.bfloat16)
        .reshape(-1, 2 * width)
    )
    coded_rows = coded.shape[0]
    padded_rows = -(-coded_rows // 16) * 16
    block = jnp.concatenate(
        [
            jnp.concatenate([keys, values], axis=1),
            jnp.pad(coded, ((0, padded_rows - coded_rows), (0, 0))),
        ],
        axis=0,
    )

    def unpack(block):
        code = block[group_size : group_size + coded_rows].reshape(3, group_size).astype(jnp.int32)
        return (
            block[:group_size, :width].reshape(group_size, local_heads, HD),
            block[:group_size, width:].reshape(group_size, local_heads, HD),
            code[0] * 128 + code[1],
            code[2],
        )

    def ring_step(state, _):
        carry, block = state
        carry, _ = attend(carry, unpack(block))
        block = lax.ppermute(block, "blk", RING[0])
        return ((carry, block), None)

    (carry, block), _ = lax.scan(ring_step, (initial, block), None, length=n_blk - 1)
    carry, _ = attend(carry, unpack(block))
    highest, denom, summed = carry
    heads_out = (summed / denom[:, :, None]).astype(jnp.bfloat16)
    heads_out = jnp.transpose(heads_out, (1, 0, 2)).reshape(group_size, width)
    heads_local = lax.all_to_all(heads_out, EXP, split_axis=0, concat_axis=0, tiled=True)
    heads_local = jnp.transpose(
        heads_local.reshape(n_exp, local_rows, width), (1, 0, 2)
    ).reshape(local_rows, n_exp * width)
    attended = jnp.dot(heads_local, output_weight, preferred_element_type=jnp.float32)
    resid_local = (stream.astype(jnp.float32) + attended).astype(jnp.bfloat16)
    normed_local = rms_norm(resid_local, post_gain)
    normed_group = lax.all_gather(normed_local, EXP, axis=0, tiled=True)
    hidden = (
        jax.nn.silu(jnp.dot(normed_group, shared_gate, preferred_element_type=jnp.float32))
        * jnp.dot(normed_group, shared_up, preferred_element_type=jnp.float32)
    ).astype(jnp.bfloat16)
    opening = jax.nn.sigmoid(
        jnp.dot(normed_group, shared_router, preferred_element_type=jnp.float32)
    )
    shared_local = lax.psum_scatter(
        (
            jnp.dot(hidden, shared_down, preferred_element_type=jnp.float32) * opening[:, None]
        ).astype(jnp.bfloat16),
        EXP,
        scatter_dimension=0,
        tiled=True,
    ).astype(jnp.float32)
    experts = lax.axis_size(CHIPS)
    capacity = -(-max(2, 5 * local_rows * TOP // (4 * experts)) // 16) * 16
    flat_ids = expert_ids.reshape(-1)
    onehot = (flat_ids[:, None] == jnp.arange(experts, dtype=jnp.int32)[None, :]).astype(jnp.int32)
    slots = jnp.sum(onehot * (jnp.cumsum(onehot, axis=0) - 1), axis=1)
    target = flat_ids * capacity + slots
    slot_ids = jnp.arange(experts * capacity, dtype=jnp.int32)
    pick = jnp.any(
        (target[None, :] == slot_ids[:, None]).reshape(experts * capacity, local_rows, TOP), axis=2
    )
    outgoing = (
        jnp.dot(pick.astype(jnp.bfloat16), normed_local, preferred_element_type=jnp.float32)
        .astype(jnp.bfloat16)
        .reshape(experts, capacity, D)
    )
    arrived = lax.all_to_all(outgoing, CHIPS, split_axis=0, concat_axis=0, tiled=True)
    arrived = lax.all_gather(arrived, "core", axis=0)
    leading = arrived.shape[:-1]
    flat_rows = arrived.reshape(-1, D)
    hidden = (
        jax.nn.silu(jnp.dot(flat_rows, expert_gate[0], preferred_element_type=jnp.float32))
        * jnp.dot(flat_rows, expert_up[0], preferred_element_type=jnp.float32)
    ).astype(jnp.bfloat16)
    half_out = (
        jnp.dot(hidden, expert_down[0], preferred_element_type=jnp.float32)
        .astype(jnp.bfloat16)
        .reshape(leading + (D,))
    )
    both_halves = lax.all_to_all(half_out, "core", split_axis=0, concat_axis=0, tiled=True)
    summed_halves = (
        both_halves[0].astype(jnp.float32) + both_halves[1].astype(jnp.float32)
    ).astype(jnp.bfloat16)
    returned = lax.all_to_all(summed_halves, CHIPS, split_axis=0, concat_axis=0, tiled=True)
    gather_pick = (target[:, None] == slot_ids[None, :]).astype(jnp.bfloat16)
    picked = jnp.dot(
        gather_pick, returned.reshape(-1, D), preferred_element_type=jnp.float32
    ) * route_weights.reshape(-1)[:, None]
    routed = jnp.sum(picked.reshape(local_rows, TOP, D), axis=1)
    routed = jnp.sum(picked.reshape(local_rows, TOP, D), axis=1)
    final = (resid_local.astype(jnp.float32) + shared_local + routed).astype(jnp.bfloat16)
    return (final, cache_keys, cache_values)


def snake(mesh):
    blk = mesh.shape["blk"]
    try:
        spots = [tuple(mesh.devices.reshape(blk, -1)[b, 0].coords) for b in range(blk)]
        zs = sorted({s[2] for s in spots})
        order = []
        for i, z in enumerate(zs):
            row = sorted((b for b in range(blk) if spots[b][2] == z), key=lambda b: spots[b][1])
            order += row if i % 2 == 0 else row[::-1]
        assert sorted(order) == list(range(blk))
    except Exception:
        order = list(range(blk))
    return [(order[k], order[(k + 1) % blk]) for k in range(blk)]


def solution(mesh):
    blk, exp = mesh.shape["blk"], mesh.shape["exp"]
    chip_mesh = Mesh(mesh.devices.reshape(blk, exp // 2, 2), ("blk", "x", "core"))
    RING[0] = snake(mesh)
    rows = ("blk",) + EXP
    in_specs = (
        P(rows, None),
        P(),
        P(None, EXP),
        P(None, EXP),
        P(None, EXP),
        P(),
        P(),
        P(None, EXP),
        P(None, EXP),
        P(EXP, None),
        P(),
        P(rows, None, None),
        P(rows, None, None),
        P(rows, None, None),
        P(rows, None),
        P(rows, None),
        P(rows),
        P(rows),
        P(rows),
    )
    out_specs = (P(rows, None), P("blk", EXP), P("blk", EXP))
    return jax.shard_map(
        per_device, mesh=chip_mesh, in_specs=in_specs, out_specs=out_specs, check_vma=False
    )
```

```python
import math

import jax
import jax.numpy as jnp
from jax import lax
from jax.sharding import Mesh, PartitionSpec as P

D = 2048
HD = 128
TOP = 4


EPS = 1e-06
FLOOR_SCORE = -1e30
EXP = ("x", "core")
CHIPS = ("blk", "x")
RING = [None]


def rms_norm(rows, gain):
    wide = rows.astype(jnp.float32)
    factor = lax.rsqrt(jnp.mean(wide * wide, axis=-1, keepdims=True) + EPS)
    return (wide * factor * gain).astype(jnp.bfloat16)


def per_device(
    stream,
    norm_gain,
    query_weight,
    key_weight,
    value_weight,
    output_weight,
    post_gain,
    shared_gate,
    shared_up,
    shared_down,
    shared_router,
    expert_gate,
    expert_up,
    expert_down,
    expert_ids,
    route_weights,
    positions,
    segment_ids,
    cache_slots,
):
    local_rows = stream.shape[0]
    n_exp = lax.axis_size(EXP)
    meta = jnp.stack([positions, segment_ids, cache_slots]).astype(jnp.int32)
    group_position, group_segment, group_slot = lax.all_gather(meta, EXP, axis=1, tiled=True)
    group_stream = lax.all_gather(stream, EXP, axis=0, tiled=True)
    group_size = group_stream.shape[0]
    normed = rms_norm(group_stream, norm_gain)
    queries = jnp.dot(normed, query_weight, preferred_element_type=jnp.float32).astype(jnp.bfloat16)
    keys = jnp.dot(normed, key_weight, preferred_element_type=jnp.float32).astype(jnp.bfloat16)
    values = jnp.dot(normed, value_weight, preferred_element_type=jnp.float32).astype(jnp.bfloat16)
    width = queries.shape[1]
    local_heads = width // HD
    cache_keys = jnp.zeros((group_size, width), jnp.bfloat16).at[group_slot].set(keys)
    cache_values = jnp.zeros((group_size, width), jnp.bfloat16).at[group_slot].set(values)
    query_heads = queries.reshape(group_size, local_heads, HD)
    factor = HD ** (-0.5)

    def attend(carry, block):
        highest, denom, summed = carry
        block_keys, block_values, block_position, block_segment = block
        scores = (
            jnp.einsum("qhd,khd->hqk", query_heads, block_keys, preferred_element_type=jnp.float32)
            * factor
        )
        allowed = (
            (block_segment[None, :] == group_segment[:, None])
            & (block_position[None, :] <= group_position[:, None])
        )[None]
        scores = jnp.where(allowed, scores, FLOOR_SCORE)
        newest = jnp.maximum(highest, jnp.max(scores, axis=2))
        probs = jnp.where(allowed, jnp.exp(scores - newest[:, :, None]), 0.0)
        shrink = jnp.exp(highest - newest)
        denom = denom * shrink + jnp.sum(probs, axis=2)
        summed = summed * shrink[:, :, None] + jnp.einsum(
            "hqk,khd->hqd",
            probs.astype(jnp.bfloat16),
            block_values,
            preferred_element_type=jnp.float32,
        )
        return ((newest, denom, summed), None)

    initial = (
        jnp.full((local_heads, group_size), FLOOR_SCORE, jnp.float32),
        jnp.zeros((local_heads, group_size), jnp.float32),
        jnp.zeros((local_heads, group_size, HD), jnp.float32),
    )
    n_blk = lax.axis_size("blk")
    coded = (
        jnp.stack([group_position // 128, group_position % 128, group_segment])
        .astype(jnp.bfloat16)
        .reshape(-1, 2 * width)
    )
    coded_rows = coded.shape[0]
    padded_rows = -(-coded_rows // 16) * 16
    block = jnp.concatenate(
        [
            jnp.concatenate([keys, values], axis=1),
            jnp.pad(coded, ((0, padded_rows - coded_rows), (0, 0))),
        ],
        axis=0,
    )

    def unpack(block):
        code = block[group_size : group_size + coded_rows].reshape(3, group_size).astype(jnp.int32)
        return (
            block[:group_size, :width].reshape(group_size, local_heads, HD),
            block[:group_size, width:].reshape(group_size, local_heads, HD),
            code[0] * 128 + code[1],
            code[2],
        )

    forward = RING[0]
    backward = [(b, a) for a, b in forward]

    def ring_step(state, _):
        carry, ahead, behind = state
        carry, _ = attend(carry, unpack(ahead))
        carry, _ = attend(carry, unpack(behind))
        ahead = lax.ppermute(ahead, "blk", forward)
        behind = lax.ppermute(behind, "blk", backward)
        return ((carry, ahead, behind), None)

    carry, _ = attend(initial, unpack(block))
    ahead = lax.ppermute(block, "blk", forward)
    behind = lax.ppermute(block, "blk", backward)
    (carry, ahead, behind), _ = lax.scan(
        ring_step, (carry, ahead, behind), None, length=n_blk // 2 - 2
    )
    opposite = lax.ppermute(ahead, "blk", forward)
    carry, _ = attend(carry, unpack(ahead))
    carry, _ = attend(carry, unpack(behind))
    carry, _ = attend(carry, unpack(opposite))
    highest, denom, summed = carry
    heads_out = (summed / denom[:, :, None]).astype(jnp.bfloat16)
    heads_out = jnp.transpose(heads_out, (1, 0, 2)).reshape(group_size, width)
    heads_local = lax.all_to_all(heads_out, EXP, split_axis=0, concat_axis=0, tiled=True)
    heads_local = jnp.transpose(
        heads_local.reshape(n_exp, local_rows, width), (1, 0, 2)
    ).reshape(local_rows, n_exp * width)
    attended = jnp.dot(heads_local, output_weight, preferred_element_type=jnp.float32)
    resid_local = (stream.astype(jnp.float32) + attended).astype(jnp.bfloat16)
    normed_local = rms_norm(resid_local, post_gain)
    normed_group = lax.all_gather(normed_local, EXP, axis=0, tiled=True)
    hidden = (
        jax.nn.silu(jnp.dot(normed_group, shared_gate, preferred_element_type=jnp.float32))
        * jnp.dot(normed_group, shared_up, preferred_element_type=jnp.float32)
    ).astype(jnp.bfloat16)
    opening = jax.nn.sigmoid(
        jnp.dot(normed_group, shared_router, preferred_element_type=jnp.float32)
    )
    shared_local = lax.psum_scatter(
        (
            jnp.dot(hidden, shared_down, preferred_element_type=jnp.float32) * opening[:, None]
        ).astype(jnp.bfloat16),
        EXP,
        scatter_dimension=0,
        tiled=True,
    ).astype(jnp.float32)
    experts = lax.axis_size(CHIPS)
    capacity = -(-max(2, 5 * local_rows * TOP // (4 * experts)) // 16) * 16
    flat_ids = expert_ids.reshape(-1)
    onehot = (flat_ids[:, None] == jnp.arange(experts, dtype=jnp.int32)[None, :]).astype(jnp.int32)
    slots = jnp.sum(onehot * (jnp.cumsum(onehot, axis=0) - 1), axis=1)
    target = flat_ids * capacity + slots
    slot_ids = jnp.arange(experts * capacity, dtype=jnp.int32)
    pick = jnp.any(
        (target[None, :] == slot_ids[:, None]).reshape(experts * capacity, local_rows, TOP), axis=2
    )
    outgoing = (
        jnp.dot(pick.astype(jnp.bfloat16), normed_local, preferred_element_type=jnp.float32)
        .astype(jnp.bfloat16)
        .reshape(experts, capacity, D)
    )
    arrived = lax.all_to_all(outgoing, CHIPS, split_axis=0, concat_axis=0, tiled=True)
    arrived = lax.all_gather(arrived, "core", axis=0)
    leading = arrived.shape[:-1]
    flat_rows = arrived.reshape(-1, D)
    hidden = (
        jax.nn.silu(jnp.dot(flat_rows, expert_gate[0], preferred_element_type=jnp.float32))
        * jnp.dot(flat_rows, expert_up[0], preferred_element_type=jnp.float32)
    ).astype(jnp.bfloat16)
    half_out = (
        jnp.dot(hidden, expert_down[0], preferred_element_type=jnp.float32)
        .astype(jnp.bfloat16)
        .reshape(leading + (D,))
    )
    both_halves = lax.all_to_all(half_out, "core", split_axis=0, concat_axis=0, tiled=True)
    summed_halves = (
        both_halves[0].astype(jnp.float32) + both_halves[1].astype(jnp.float32)
    ).astype(jnp.bfloat16)
    returned = lax.all_to_all(summed_halves, CHIPS, split_axis=0, concat_axis=0, tiled=True)
    gather_pick = (target[:, None] == slot_ids[None, :]).astype(jnp.bfloat16)
    picked = jnp.dot(
        gather_pick, returned.reshape(-1, D), preferred_element_type=jnp.float32
    ) * route_weights.reshape(-1)[:, None]
    routed = jnp.sum(picked.reshape(local_rows, TOP, D), axis=1)
    routed = jnp.sum(picked.reshape(local_rows, TOP, D), axis=1)
    final = (resid_local.astype(jnp.float32) + shared_local + routed).astype(jnp.bfloat16)
    return (final, cache_keys, cache_values)


def snake(mesh):
    blk = mesh.shape["blk"]
    try:
        spots = [tuple(mesh.devices.reshape(blk, -1)[b, 0].coords) for b in range(blk)]
        zs = sorted({s[2] for s in spots})
        order = []
        for i, z in enumerate(zs):
            row = sorted((b for b in range(blk) if spots[b][2] == z), key=lambda b: spots[b][1])
            order += row if i % 2 == 0 else row[::-1]
        assert sorted(order) == list(range(blk))
    except Exception:
        order = list(range(blk))
    return [(order[k], order[(k + 1) % blk]) for k in range(blk)]


def solution(mesh):
    blk, exp = mesh.shape["blk"], mesh.shape["exp"]
    chip_mesh = Mesh(mesh.devices.reshape(blk, exp // 2, 2), ("blk", "x", "core"))
    RING[0] = snake(mesh)
    rows = ("blk",) + EXP
    in_specs = (
        P(rows, None),
        P(),
        P(None, EXP),
        P(None, EXP),
        P(None, EXP),
        P(),
        P(),
        P(None, EXP),
        P(None, EXP),
        P(EXP, None),
        P(),
        P(rows, None, None),
        P(rows, None, None),
        P(rows, None, None),
        P(rows, None),
        P(rows, None),
        P(rows),
        P(rows),
        P(rows),
    )
    out_specs = (P(rows, None), P("blk", EXP), P("blk", EXP))
    return jax.shard_map(
        per_device, mesh=chip_mesh, in_specs=in_specs, out_specs=out_specs, check_vma=False
    )
```

```python
import math

import jax
import jax.numpy as jnp
from jax import lax
from jax.sharding import Mesh, PartitionSpec as P

D = 2048
HD = 128
TOP = 4


EPS = 1e-06
FLOOR_SCORE = -1e30
EXP = ("x", "core")
CHIPS = ("blk", "x")
RING = [None]


def rms_norm(rows, gain):
    wide = rows.astype(jnp.float32)
    factor = lax.rsqrt(jnp.mean(wide * wide, axis=-1, keepdims=True) + EPS)
    return (wide * factor * gain).astype(jnp.bfloat16)


def per_device(
    stream,
    norm_gain,
    query_weight,
    key_weight,
    value_weight,
    output_weight,
    post_gain,
    shared_gate,
    shared_up,
    shared_down,
    shared_router,
    expert_gate,
    expert_up,
    expert_down,
    expert_ids,
    route_weights,
    positions,
    segment_ids,
    cache_slots,
):
    local_rows = stream.shape[0]
    n_exp = lax.axis_size(EXP)
    meta = jnp.stack([positions, segment_ids, cache_slots]).astype(jnp.int32)
    group_position, group_segment, group_slot = lax.all_gather(meta, EXP, axis=1, tiled=True)
    group_stream = lax.all_gather(stream, EXP, axis=0, tiled=True)
    group_size = group_stream.shape[0]
    normed = rms_norm(group_stream, norm_gain)
    queries = jnp.dot(normed, query_weight, preferred_element_type=jnp.float32).astype(jnp.bfloat16)
    keys = jnp.dot(normed, key_weight, preferred_element_type=jnp.float32).astype(jnp.bfloat16)
    values = jnp.dot(normed, value_weight, preferred_element_type=jnp.float32).astype(jnp.bfloat16)
    width = queries.shape[1]
    local_heads = width // HD
    cache_keys = jnp.zeros((group_size, width), jnp.bfloat16).at[group_slot].set(keys)
    cache_values = jnp.zeros((group_size, width), jnp.bfloat16).at[group_slot].set(values)
    query_heads = queries.reshape(group_size, local_heads, HD)
    factor = HD ** (-0.5)

    def attend(carry, block):
        highest, denom, summed = carry
        block_keys, block_values, block_position, block_segment = block
        scores = (
            jnp.einsum("qhd,khd->hqk", query_heads, block_keys, preferred_element_type=jnp.float32)
            * factor
        )
        allowed = (
            (block_segment[None, :] == group_segment[:, None])
            & (block_position[None, :] <= group_position[:, None])
        )[None]
        scores = jnp.where(allowed, scores, FLOOR_SCORE)
        newest = jnp.maximum(highest, jnp.max(scores, axis=2))
        probs = jnp.where(allowed, jnp.exp(scores - newest[:, :, None]), 0.0)
        shrink = jnp.exp(highest - newest)
        denom = denom * shrink + jnp.sum(probs, axis=2)
        summed = summed * shrink[:, :, None] + jnp.einsum(
            "hqk,khd->hqd",
            probs.astype(jnp.bfloat16),
            block_values,
            preferred_element_type=jnp.float32,
        )
        return ((newest, denom, summed), None)

    initial = (
        jnp.full((local_heads, group_size), FLOOR_SCORE, jnp.float32),
        jnp.zeros((local_heads, group_size), jnp.float32),
        jnp.zeros((local_heads, group_size, HD), jnp.float32),
    )
    n_blk = lax.axis_size("blk")
    coded = (
        jnp.stack([group_position // 128, group_position % 128, group_segment])
        .astype(jnp.bfloat16)
        .reshape(-1, 2 * width)
    )
    coded_rows = coded.shape[0]
    padded_rows = -(-coded_rows // 16) * 16
    block = jnp.concatenate(
        [
            jnp.concatenate([keys, values], axis=1),
            jnp.pad(coded, ((0, padded_rows - coded_rows), (0, 0))),
        ],
        axis=0,
    )

    def unpack(block):
        code = block[group_size : group_size + coded_rows].reshape(3, group_size).astype(jnp.int32)
        return (
            block[:group_size, :width].reshape(group_size, local_heads, HD),
            block[:group_size, width:].reshape(group_size, local_heads, HD),
            code[0] * 128 + code[1],
            code[2],
        )

    forward = RING[0]
    backward = [(b, a) for a, b in forward]

    def ring_step(state, _):
        carry, ahead, behind = state
        carry, _ = attend(carry, unpack(ahead))
        carry, _ = attend(carry, unpack(behind))
        ahead = lax.ppermute(ahead, "blk", forward)
        behind = lax.ppermute(behind, "blk", backward)
        return ((carry, ahead, behind), None)

    carry, _ = attend(initial, unpack(block))
    ahead = lax.ppermute(block, "blk", forward)
    behind = lax.ppermute(block, "blk", backward)
    (carry, ahead, behind), _ = lax.scan(
        ring_step, (carry, ahead, behind), None, length=n_blk // 2 - 2
    )
    opposite = lax.ppermute(ahead, "blk", forward)
    carry, _ = attend(carry, unpack(ahead))
    carry, _ = attend(carry, unpack(behind))
    carry, _ = attend(carry, unpack(opposite))
    highest, denom, summed = carry
    heads_out = (summed / denom[:, :, None]).astype(jnp.bfloat16)
    heads_out = jnp.transpose(heads_out, (1, 0, 2)).reshape(group_size, width)
    heads_local = lax.all_to_all(heads_out, EXP, split_axis=0, concat_axis=0, tiled=True)
    heads_local = jnp.transpose(
        heads_local.reshape(n_exp, local_rows, width), (1, 0, 2)
    ).reshape(local_rows, n_exp * width)
    attended = jnp.dot(heads_local, output_weight, preferred_element_type=jnp.float32)
    resid_local = (stream.astype(jnp.float32) + attended).astype(jnp.bfloat16)
    normed_local = rms_norm(resid_local, post_gain)
    normed_group = lax.all_gather(normed_local, EXP, axis=0, tiled=True)
    hidden = (
        jax.nn.silu(jnp.dot(normed_group, shared_gate, preferred_element_type=jnp.float32))
        * jnp.dot(normed_group, shared_up, preferred_element_type=jnp.float32)
    ).astype(jnp.bfloat16)
    opening = jax.nn.sigmoid(
        jnp.dot(normed_group, shared_router, preferred_element_type=jnp.float32)
    )
    shared_local = lax.psum_scatter(
        (
            jnp.dot(hidden, shared_down, preferred_element_type=jnp.float32) * opening[:, None]
        ).astype(jnp.bfloat16),
        EXP,
        scatter_dimension=0,
        tiled=True,
    ).astype(jnp.float32)
    experts = lax.axis_size(CHIPS)
    capacity = -(-max(2, 5 * local_rows * TOP // (4 * experts)) // 16) * 16
    flat_ids = expert_ids.reshape(-1)
    onehot = (flat_ids[:, None] == jnp.arange(experts, dtype=jnp.int32)[None, :]).astype(jnp.int32)
    slots = jnp.sum(onehot * (jnp.cumsum(onehot, axis=0) - 1), axis=1)
    target = flat_ids * capacity + slots
    slot_ids = jnp.arange(experts * capacity, dtype=jnp.int32)
    pick = jnp.any(
        (target[None, :] == slot_ids[:, None]).reshape(experts * capacity, local_rows, TOP), axis=2
    )
    outgoing = (
        jnp.dot(pick.astype(jnp.bfloat16), normed_local, preferred_element_type=jnp.float32)
        .astype(jnp.bfloat16)
        .reshape(experts, capacity, D)
    )
    arrived = lax.all_to_all(outgoing, CHIPS, split_axis=0, concat_axis=0, tiled=True)
    arrived = lax.all_gather(arrived, "core", axis=0)
    leading = arrived.shape[:-1]
    flat_rows = arrived.reshape(-1, D)
    hidden = (
        jax.nn.silu(jnp.dot(flat_rows, expert_gate[0], preferred_element_type=jnp.float32))
        * jnp.dot(flat_rows, expert_up[0], preferred_element_type=jnp.float32)
    ).astype(jnp.bfloat16)
    half_out = (
        jnp.dot(hidden, expert_down[0], preferred_element_type=jnp.float32)
        .astype(jnp.bfloat16)
        .reshape(leading + (D,))
    )
    both_halves = lax.all_to_all(half_out, "core", split_axis=0, concat_axis=0, tiled=True)
    summed_halves = (
        both_halves[0].astype(jnp.float32) + both_halves[1].astype(jnp.float32)
    ).astype(jnp.bfloat16)
    returned = lax.all_to_all(summed_halves, CHIPS, split_axis=0, concat_axis=0, tiled=True)
    choice_weights = jnp.sum(
        jnp.where(
            target.reshape(local_rows, TOP, 1) == slot_ids[None, None, :],
            route_weights[:, :, None],
            0.0,
        ),
        axis=1,
    )
    routed = jnp.dot(
        choice_weights,
        returned.reshape(-1, D).astype(jnp.float32),
        precision=lax.Precision.HIGHEST,
        preferred_element_type=jnp.float32,
    )
    final = (resid_local.astype(jnp.float32) + shared_local + routed).astype(jnp.bfloat16)
    return (final, cache_keys, cache_values)


def snake(mesh):
    blk = mesh.shape["blk"]
    try:
        spots = [tuple(mesh.devices.reshape(blk, -1)[b, 0].coords) for b in range(blk)]
        zs = sorted({s[2] for s in spots})
        order = []
        for i, z in enumerate(zs):
            row = sorted((b for b in range(blk) if spots[b][2] == z), key=lambda b: spots[b][1])
            order += row if i % 2 == 0 else row[::-1]
        assert sorted(order) == list(range(blk))
    except Exception:
        order = list(range(blk))
    return [(order[k], order[(k + 1) % blk]) for k in range(blk)]


def solution(mesh):
    blk, exp = mesh.shape["blk"], mesh.shape["exp"]
    chip_mesh = Mesh(mesh.devices.reshape(blk, exp // 2, 2), ("blk", "x", "core"))
    RING[0] = snake(mesh)
    rows = ("blk",) + EXP
    in_specs = (
        P(rows, None),
        P(),
        P(None, EXP),
        P(None, EXP),
        P(None, EXP),
        P(),
        P(),
        P(None, EXP),
        P(None, EXP),
        P(EXP, None),
        P(),
        P(rows, None, None),
        P(rows, None, None),
        P(rows, None, None),
        P(rows, None),
        P(rows, None),
        P(rows),
        P(rows),
        P(rows),
    )
    out_specs = (P(rows, None), P("blk", EXP), P("blk", EXP))
    return jax.shard_map(
        per_device, mesh=chip_mesh, in_specs=in_specs, out_specs=out_specs, check_vma=False
    )
```

```python
import math

import jax
import jax.numpy as jnp
from jax import lax
from jax.sharding import Mesh, PartitionSpec as P

D = 2048
HD = 128
TOP = 4


EPS = 1e-06
FLOOR_SCORE = -1e30
EXP = ("x", "core")
CHIPS = ("blk", "x")
RING = [None]


def rms_norm(rows, gain):
    wide = rows.astype(jnp.float32)
    factor = lax.rsqrt(jnp.mean(wide * wide, axis=-1, keepdims=True) + EPS)
    return (wide * factor * gain).astype(jnp.bfloat16)


def per_device(
    stream,
    norm_gain,
    query_weight,
    key_weight,
    value_weight,
    output_weight,
    post_gain,
    shared_gate,
    shared_up,
    shared_down,
    shared_router,
    expert_gate,
    expert_up,
    expert_down,
    expert_ids,
    route_weights,
    positions,
    segment_ids,
    cache_slots,
):
    local_rows = stream.shape[0]
    n_exp = lax.axis_size(EXP)
    meta = jnp.stack([positions, segment_ids, cache_slots]).astype(jnp.int32)
    group_position, group_segment, group_slot = lax.all_gather(meta, EXP, axis=1, tiled=True)
    group_stream = lax.all_gather(stream, EXP, axis=0, tiled=True)
    group_size = group_stream.shape[0]
    normed = rms_norm(group_stream, norm_gain)
    queries = jnp.dot(normed, query_weight, preferred_element_type=jnp.float32).astype(jnp.bfloat16)
    keys = jnp.dot(normed, key_weight, preferred_element_type=jnp.float32).astype(jnp.bfloat16)
    values = jnp.dot(normed, value_weight, preferred_element_type=jnp.float32).astype(jnp.bfloat16)
    width = queries.shape[1]
    local_heads = width // HD
    cache_keys = jnp.zeros((group_size, width), jnp.bfloat16).at[group_slot].set(keys)
    cache_values = jnp.zeros((group_size, width), jnp.bfloat16).at[group_slot].set(values)
    query_heads = queries.reshape(group_size, local_heads, HD)
    factor = HD ** (-0.5)

    def attend(carry, block):
        highest, denom, summed = carry
        block_keys, block_values, block_position, block_segment = block
        scores = (
            jnp.einsum("qhd,khd->hqk", query_heads, block_keys, preferred_element_type=jnp.float32)
            * factor
        )
        allowed = (
            (block_segment[None, :] == group_segment[:, None])
            & (block_position[None, :] <= group_position[:, None])
        )[None]
        scores = jnp.where(allowed, scores, FLOOR_SCORE)
        newest = jnp.maximum(highest, jnp.max(scores, axis=2))
        probs = jnp.where(allowed, jnp.exp(scores - newest[:, :, None]), 0.0)
        shrink = jnp.exp(highest - newest)
        denom = denom * shrink + jnp.sum(probs, axis=2)
        summed = summed * shrink[:, :, None] + jnp.einsum(
            "hqk,khd->hqd",
            probs.astype(jnp.bfloat16),
            block_values,
            preferred_element_type=jnp.float32,
        )
        return ((newest, denom, summed), None)

    initial = (
        jnp.full((local_heads, group_size), FLOOR_SCORE, jnp.float32),
        jnp.zeros((local_heads, group_size), jnp.float32),
        jnp.zeros((local_heads, group_size, HD), jnp.float32),
    )
    n_blk = lax.axis_size("blk")
    coded = (
        jnp.stack([group_position // 128, group_position % 128, group_segment])
        .astype(jnp.bfloat16)
        .reshape(-1, 2 * width)
    )
    coded_rows = coded.shape[0]
    padded_rows = -(-coded_rows // 16) * 16
    block = jnp.concatenate(
        [
            jnp.concatenate([keys, values], axis=1),
            jnp.pad(coded, ((0, padded_rows - coded_rows), (0, 0))),
        ],
        axis=0,
    )

    def unpack(block):
        code = block[group_size : group_size + coded_rows].reshape(3, group_size).astype(jnp.int32)
        return (
            block[:group_size, :width].reshape(group_size, local_heads, HD),
            block[:group_size, width:].reshape(group_size, local_heads, HD),
            code[0] * 128 + code[1],
            code[2],
        )

    forward = RING[0]
    backward = [(b, a) for a, b in forward]

    def ring_step(state, _):
        carry, ahead, behind = state
        carry, _ = attend(carry, unpack(ahead))
        carry, _ = attend(carry, unpack(behind))
        ahead = lax.ppermute(ahead, "blk", forward)
        behind = lax.ppermute(behind, "blk", backward)
        return ((carry, ahead, behind), None)

    carry, _ = attend(initial, unpack(block))
    ahead = lax.ppermute(block, "blk", forward)
    behind = lax.ppermute(block, "blk", backward)
    state = (carry, ahead, behind)
    for _ in range(n_blk // 2 - 2):
        state, _ = ring_step(state, None)
    carry, ahead, behind = state
    opposite = lax.ppermute(ahead, "blk", forward)
    carry, _ = attend(carry, unpack(ahead))
    carry, _ = attend(carry, unpack(behind))
    carry, _ = attend(carry, unpack(opposite))
    highest, denom, summed = carry
    heads_out = (summed / denom[:, :, None]).astype(jnp.bfloat16)
    heads_out = jnp.transpose(heads_out, (1, 0, 2)).reshape(group_size, width)
    heads_local = lax.all_to_all(heads_out, EXP, split_axis=0, concat_axis=0, tiled=True)
    heads_local = jnp.transpose(
        heads_local.reshape(n_exp, local_rows, width), (1, 0, 2)
    ).reshape(local_rows, n_exp * width)
    attended = jnp.dot(heads_local, output_weight, preferred_element_type=jnp.float32)
    resid_local = (stream.astype(jnp.float32) + attended).astype(jnp.bfloat16)
    normed_local = rms_norm(resid_local, post_gain)
    normed_group = lax.all_gather(normed_local, EXP, axis=0, tiled=True)
    hidden = (
        jax.nn.silu(jnp.dot(normed_group, shared_gate, preferred_element_type=jnp.float32))
        * jnp.dot(normed_group, shared_up, preferred_element_type=jnp.float32)
    ).astype(jnp.bfloat16)
    opening = jax.nn.sigmoid(
        jnp.dot(normed_group, shared_router, preferred_element_type=jnp.float32)
    )
    shared_local = lax.psum_scatter(
        (
            jnp.dot(hidden, shared_down, preferred_element_type=jnp.float32) * opening[:, None]
        ).astype(jnp.bfloat16),
        EXP,
        scatter_dimension=0,
        tiled=True,
    ).astype(jnp.float32)
    experts = lax.axis_size(CHIPS)
    capacity = -(-max(2, 5 * local_rows * TOP // (4 * experts)) // 16) * 16
    flat_ids = expert_ids.reshape(-1)
    onehot = (flat_ids[:, None] == jnp.arange(experts, dtype=jnp.int32)[None, :]).astype(jnp.int32)
    slots = jnp.sum(onehot * (jnp.cumsum(onehot, axis=0) - 1), axis=1)
    target = flat_ids * capacity + slots
    slot_ids = jnp.arange(experts * capacity, dtype=jnp.int32)
    pick = jnp.any(
        (target[None, :] == slot_ids[:, None]).reshape(experts * capacity, local_rows, TOP), axis=2
    )
    outgoing = (
        jnp.dot(pick.astype(jnp.bfloat16), normed_local, preferred_element_type=jnp.float32)
        .astype(jnp.bfloat16)
        .reshape(experts, capacity, D)
    )
    arrived = lax.all_to_all(outgoing, CHIPS, split_axis=0, concat_axis=0, tiled=True)
    arrived = lax.all_gather(arrived, "core", axis=0)
    leading = arrived.shape[:-1]
    flat_rows = arrived.reshape(-1, D)
    hidden = (
        jax.nn.silu(jnp.dot(flat_rows, expert_gate[0], preferred_element_type=jnp.float32))
        * jnp.dot(flat_rows, expert_up[0], preferred_element_type=jnp.float32)
    ).astype(jnp.bfloat16)
    half_out = (
        jnp.dot(hidden, expert_down[0], preferred_element_type=jnp.float32)
        .astype(jnp.bfloat16)
        .reshape(leading + (D,))
    )
    both_halves = lax.all_to_all(half_out, "core", split_axis=0, concat_axis=0, tiled=True)
    summed_halves = (
        both_halves[0].astype(jnp.float32) + both_halves[1].astype(jnp.float32)
    ).astype(jnp.bfloat16)
    returned = lax.all_to_all(summed_halves, CHIPS, split_axis=0, concat_axis=0, tiled=True)
    choice_weights = jnp.sum(
        jnp.where(
            target.reshape(local_rows, TOP, 1) == slot_ids[None, None, :],
            route_weights[:, :, None],
            0.0,
        ),
        axis=1,
    )
    routed = jnp.dot(
        choice_weights,
        returned.reshape(-1, D).astype(jnp.float32),
        precision=lax.Precision.HIGHEST,
        preferred_element_type=jnp.float32,
    )
    final = (resid_local.astype(jnp.float32) + shared_local + routed).astype(jnp.bfloat16)
    return (final, cache_keys, cache_values)


def snake(mesh):
    blk = mesh.shape["blk"]
    try:
        spots = [tuple(mesh.devices.reshape(blk, -1)[b, 0].coords) for b in range(blk)]
        zs = sorted({s[2] for s in spots})
        order = []
        for i, z in enumerate(zs):
            row = sorted((b for b in range(blk) if spots[b][2] == z), key=lambda b: spots[b][1])
            order += row if i % 2 == 0 else row[::-1]
        assert sorted(order) == list(range(blk))
    except Exception:
        order = list(range(blk))
    return [(order[k], order[(k + 1) % blk]) for k in range(blk)]


def solution(mesh):
    blk, exp = mesh.shape["blk"], mesh.shape["exp"]
    chip_mesh = Mesh(mesh.devices.reshape(blk, exp // 2, 2), ("blk", "x", "core"))
    RING[0] = snake(mesh)
    rows = ("blk",) + EXP
    in_specs = (
        P(rows, None),
        P(),
        P(None, EXP),
        P(None, EXP),
        P(None, EXP),
        P(),
        P(),
        P(None, EXP),
        P(None, EXP),
        P(EXP, None),
        P(),
        P(rows, None, None),
        P(rows, None, None),
        P(rows, None, None),
        P(rows, None),
        P(rows, None),
        P(rows),
        P(rows),
        P(rows),
    )
    out_specs = (P(rows, None), P("blk", EXP), P("blk", EXP))
    return jax.shard_map(
        per_device, mesh=chip_mesh, in_specs=in_specs, out_specs=out_specs, check_vma=False
    )
```

```python
import math

import jax
import jax.numpy as jnp
from jax import lax
from jax.sharding import Mesh, PartitionSpec as P

D = 2048
HD = 128
TOP = 4


EPS = 1e-06
FLOOR_SCORE = -1e30
EXP = ("x", "core")
CHIPS = ("blk", "x")
RING = [None]


def rms_norm(rows, gain):
    wide = rows.astype(jnp.float32)
    factor = lax.rsqrt(jnp.mean(wide * wide, axis=-1, keepdims=True) + EPS)
    return (wide * factor * gain).astype(jnp.bfloat16)


def per_device(
    stream,
    norm_gain,
    query_weight,
    key_weight,
    value_weight,
    output_weight,
    post_gain,
    shared_gate,
    shared_up,
    shared_down,
    shared_router,
    expert_gate,
    expert_up,
    expert_down,
    expert_ids,
    route_weights,
    positions,
    segment_ids,
    cache_slots,
):
    local_rows = stream.shape[0]
    n_exp = lax.axis_size(EXP)
    meta = jnp.stack([positions, segment_ids, cache_slots]).astype(jnp.int32)
    group_position, group_segment, group_slot = lax.all_gather(meta, EXP, axis=1, tiled=True)
    group_stream = lax.all_gather(stream, EXP, axis=0, tiled=True)
    group_size = group_stream.shape[0]
    normed = rms_norm(group_stream, norm_gain)
    queries = jnp.dot(normed, query_weight, preferred_element_type=jnp.float32).astype(jnp.bfloat16)
    keys = jnp.dot(normed, key_weight, preferred_element_type=jnp.float32).astype(jnp.bfloat16)
    values = jnp.dot(normed, value_weight, preferred_element_type=jnp.float32).astype(jnp.bfloat16)
    width = queries.shape[1]
    local_heads = width // HD
    cache_keys = jnp.zeros((group_size, width), jnp.bfloat16).at[group_slot].set(keys)
    cache_values = jnp.zeros((group_size, width), jnp.bfloat16).at[group_slot].set(values)
    query_heads = queries.reshape(group_size, local_heads, HD)
    factor = HD ** (-0.5)

    def attend(carry, block):
        highest, denom, summed = carry
        block_keys, block_values, block_position, block_segment = block
        scores = (
            jnp.einsum("qhd,khd->hqk", query_heads, block_keys, preferred_element_type=jnp.float32)
            * factor
        )
        allowed = (
            (block_segment[None, :] == group_segment[:, None])
            & (block_position[None, :] <= group_position[:, None])
        )[None]
        scores = jnp.where(allowed, scores, FLOOR_SCORE)
        newest = jnp.maximum(highest, jnp.max(scores, axis=2))
        probs = jnp.where(allowed, jnp.exp(scores - newest[:, :, None]), 0.0)
        shrink = jnp.exp(highest - newest)
        denom = denom * shrink + jnp.sum(probs, axis=2)
        summed = summed * shrink[:, :, None] + jnp.einsum(
            "hqk,khd->hqd",
            probs.astype(jnp.bfloat16),
            block_values,
            preferred_element_type=jnp.float32,
        )
        return ((newest, denom, summed), None)

    initial = (
        jnp.full((local_heads, group_size), FLOOR_SCORE, jnp.float32),
        jnp.zeros((local_heads, group_size), jnp.float32),
        jnp.zeros((local_heads, group_size, HD), jnp.float32),
    )
    n_blk = lax.axis_size("blk")
    coded = (
        jnp.stack([group_position // 128, group_position % 128, group_segment])
        .astype(jnp.bfloat16)
        .reshape(-1, 2 * width)
    )
    coded_rows = coded.shape[0]
    padded_rows = -(-coded_rows // 16) * 16
    block = jnp.concatenate(
        [
            jnp.concatenate([keys, values], axis=1),
            jnp.pad(coded, ((0, padded_rows - coded_rows), (0, 0))),
        ],
        axis=0,
    )

    def unpack(block):
        code = block[group_size : group_size + coded_rows].reshape(3, group_size).astype(jnp.int32)
        return (
            block[:group_size, :width].reshape(group_size, local_heads, HD),
            block[:group_size, width:].reshape(group_size, local_heads, HD),
            code[0] * 128 + code[1],
            code[2],
        )

    forward = RING[0]
    backward = [(b, a) for a, b in forward]

    def ring_step(state, _):
        carry, ahead, behind = state
        carry, _ = attend(carry, unpack(ahead))
        carry, _ = attend(carry, unpack(behind))
        ahead = lax.ppermute(ahead, "blk", forward)
        behind = lax.ppermute(behind, "blk", backward)
        return ((carry, ahead, behind), None)

    carry, _ = attend(initial, unpack(block))
    ahead = lax.ppermute(block, "blk", forward)
    behind = lax.ppermute(block, "blk", backward)
    (carry, ahead, behind), _ = lax.scan(
        ring_step, (carry, ahead, behind), None, length=n_blk // 2 - 2
    )
    opposite = lax.ppermute(ahead, "blk", forward)
    carry, _ = attend(carry, unpack(ahead))
    carry, _ = attend(carry, unpack(behind))
    carry, _ = attend(carry, unpack(opposite))
    highest, denom, summed = carry
    heads_out = (summed / denom[:, :, None]).astype(jnp.bfloat16)
    heads_out = jnp.transpose(heads_out, (1, 0, 2)).reshape(group_size, width)
    heads_local = lax.all_to_all(heads_out, EXP, split_axis=0, concat_axis=0, tiled=True)
    heads_local = jnp.transpose(
        heads_local.reshape(n_exp, local_rows, width), (1, 0, 2)
    ).reshape(local_rows, n_exp * width)
    attended = jnp.dot(heads_local, output_weight, preferred_element_type=jnp.float32)
    resid_local = (stream.astype(jnp.float32) + attended).astype(jnp.bfloat16)
    normed_local = rms_norm(resid_local, post_gain)
    normed_group = lax.all_gather(normed_local, EXP, axis=0, tiled=True)
    hidden = (
        jax.nn.silu(jnp.dot(normed_group, shared_gate, preferred_element_type=jnp.float32))
        * jnp.dot(normed_group, shared_up, preferred_element_type=jnp.float32)
    ).astype(jnp.bfloat16)
    opening = jax.nn.sigmoid(
        jnp.dot(normed_group, shared_router, preferred_element_type=jnp.float32)
    )
    shared_local = lax.psum_scatter(
        (
            jnp.dot(hidden, shared_down, preferred_element_type=jnp.float32) * opening[:, None]
        ).astype(jnp.bfloat16),
        EXP,
        scatter_dimension=0,
        tiled=True,
    ).astype(jnp.float32)
    experts = lax.axis_size(CHIPS)
    capacity = -(-max(2, 5 * local_rows * TOP // (4 * experts)) // 16) * 16
    flat_ids = expert_ids.reshape(-1)
    onehot = (flat_ids[:, None] == jnp.arange(experts, dtype=jnp.int32)[None, :]).astype(jnp.int32)
    slots = jnp.sum(onehot * (jnp.cumsum(onehot, axis=0) - 1), axis=1)
    target = flat_ids * capacity + slots
    slot_ids = jnp.arange(experts * capacity, dtype=jnp.int32)
    pick = jnp.any(
        (target[None, :] == slot_ids[:, None]).reshape(experts * capacity, local_rows, TOP), axis=2
    )
    outgoing = (
        jnp.dot(pick.astype(jnp.bfloat16), normed_local, preferred_element_type=jnp.float32)
        .astype(jnp.bfloat16)
        .reshape(experts, capacity, D)
    )
    arrived = lax.all_to_all(outgoing, CHIPS, split_axis=0, concat_axis=0, tiled=True)
    arrived = lax.all_gather(arrived, "core", axis=0)
    leading = arrived.shape[:-1]
    flat_rows = arrived.reshape(-1, D)
    hidden = (
        jax.nn.silu(jnp.dot(flat_rows, expert_gate[0], preferred_element_type=jnp.float32))
        * jnp.dot(flat_rows, expert_up[0], preferred_element_type=jnp.float32)
    ).astype(jnp.bfloat16)
    half_out = (
        jnp.dot(hidden, expert_down[0], preferred_element_type=jnp.float32)
        .astype(jnp.bfloat16)
        .reshape(leading + (D,))
    )
    both_halves = lax.all_to_all(half_out, "core", split_axis=0, concat_axis=0, tiled=True)
    summed_halves = (
        both_halves[0].astype(jnp.float32) + both_halves[1].astype(jnp.float32)
    ).astype(jnp.bfloat16)
    returned = lax.all_to_all(summed_halves, CHIPS, split_axis=0, concat_axis=0, tiled=True)
    target_by_choice = target.reshape(local_rows, TOP).T.reshape(-1)
    gather_pick = (target_by_choice[:, None] == slot_ids[None, :]).astype(jnp.bfloat16)
    picked = jnp.dot(
        gather_pick, returned.reshape(-1, D), preferred_element_type=jnp.float32
    ) * route_weights.T.reshape(-1)[:, None]
    routed = jnp.sum(picked.reshape(TOP, local_rows, D), axis=0)
    final = (resid_local.astype(jnp.float32) + shared_local + routed).astype(jnp.bfloat16)
    return (final, cache_keys, cache_values)


def snake(mesh):
    blk = mesh.shape["blk"]
    try:
        spots = [tuple(mesh.devices.reshape(blk, -1)[b, 0].coords) for b in range(blk)]
        zs = sorted({s[2] for s in spots})
        order = []
        for i, z in enumerate(zs):
            row = sorted((b for b in range(blk) if spots[b][2] == z), key=lambda b: spots[b][1])
            order += row if i % 2 == 0 else row[::-1]
        assert sorted(order) == list(range(blk))
    except Exception:
        order = list(range(blk))
    return [(order[k], order[(k + 1) % blk]) for k in range(blk)]


def solution(mesh):
    blk, exp = mesh.shape["blk"], mesh.shape["exp"]
    chip_mesh = Mesh(mesh.devices.reshape(blk, exp // 2, 2), ("blk", "x", "core"))
    RING[0] = snake(mesh)
    rows = ("blk",) + EXP
    in_specs = (
        P(rows, None),
        P(),
        P(None, EXP),
        P(None, EXP),
        P(None, EXP),
        P(),
        P(),
        P(None, EXP),
        P(None, EXP),
        P(EXP, None),
        P(),
        P(rows, None, None),
        P(rows, None, None),
        P(rows, None, None),
        P(rows, None),
        P(rows, None),
        P(rows),
        P(rows),
        P(rows),
    )
    out_specs = (P(rows, None), P("blk", EXP), P("blk", EXP))
    return jax.shard_map(
        per_device, mesh=chip_mesh, in_specs=in_specs, out_specs=out_specs, check_vma=False
    )
```

```python
import math

import jax
import jax.numpy as jnp
from jax import lax
from jax.sharding import Mesh, PartitionSpec as P

D = 2048
HD = 128
TOP = 4


EPS = 1e-06
FLOOR_SCORE = -1e30
EXP = ("x", "core")
CHIPS = ("blk", "x")
RING = [None]


def rms_norm(rows, gain):
    wide = rows.astype(jnp.float32)
    factor = lax.rsqrt(jnp.mean(wide * wide, axis=-1, keepdims=True) + EPS)
    return (wide * factor * gain).astype(jnp.bfloat16)


def per_device(
    stream,
    norm_gain,
    query_weight,
    key_weight,
    value_weight,
    output_weight,
    post_gain,
    shared_gate,
    shared_up,
    shared_down,
    shared_router,
    expert_gate,
    expert_up,
    expert_down,
    expert_ids,
    route_weights,
    positions,
    segment_ids,
    cache_slots,
):
    local_rows = stream.shape[0]
    n_exp = lax.axis_size(EXP)
    meta = jnp.stack([positions, segment_ids, cache_slots]).astype(jnp.int32)
    group_position, group_segment, group_slot = lax.all_gather(meta, EXP, axis=1, tiled=True)
    group_stream = lax.all_gather(stream, EXP, axis=0, tiled=True)
    group_size = group_stream.shape[0]
    normed = rms_norm(group_stream, norm_gain)
    queries = jnp.dot(normed, query_weight, preferred_element_type=jnp.float32).astype(jnp.bfloat16)
    keys = jnp.dot(normed, key_weight, preferred_element_type=jnp.float32).astype(jnp.bfloat16)
    values = jnp.dot(normed, value_weight, preferred_element_type=jnp.float32).astype(jnp.bfloat16)
    width = queries.shape[1]
    local_heads = width // HD
    cache_keys = jnp.zeros((group_size, width), jnp.bfloat16).at[group_slot].set(keys)
    cache_values = jnp.zeros((group_size, width), jnp.bfloat16).at[group_slot].set(values)
    query_heads = queries.reshape(group_size, local_heads, HD)
    factor = HD ** (-0.5)

    def attend(carry, block):
        highest, denom, summed = carry
        block_keys, block_values, block_position, block_segment = block
        scores = (
            jnp.einsum("qhd,khd->hqk", query_heads, block_keys, preferred_element_type=jnp.float32)
            * factor
        )
        allowed = (
            (block_segment[None, :] == group_segment[:, None])
            & (block_position[None, :] <= group_position[:, None])
        )[None]
        scores = jnp.where(allowed, scores, FLOOR_SCORE)
        newest = jnp.maximum(highest, jnp.max(scores, axis=2))
        probs = jnp.where(allowed, jnp.exp(scores - newest[:, :, None]), 0.0)
        shrink = jnp.exp(highest - newest)
        denom = denom * shrink + jnp.sum(probs, axis=2)
        summed = summed * shrink[:, :, None] + jnp.einsum(
            "hqk,khd->hqd",
            probs.astype(jnp.bfloat16),
            block_values,
            preferred_element_type=jnp.float32,
        )
        return ((newest, denom, summed), None)

    initial = (
        jnp.full((local_heads, group_size), FLOOR_SCORE, jnp.float32),
        jnp.zeros((local_heads, group_size), jnp.float32),
        jnp.zeros((local_heads, group_size, HD), jnp.float32),
    )
    n_blk = lax.axis_size("blk")
    coded = (
        jnp.stack([group_position // 128, group_position % 128, group_segment])
        .astype(jnp.bfloat16)
        .reshape(-1, 2 * width)
    )
    coded_rows = coded.shape[0]
    padded_rows = -(-coded_rows // 16) * 16
    block = jnp.concatenate(
        [
            jnp.concatenate([keys, values], axis=1),
            jnp.pad(coded, ((0, padded_rows - coded_rows), (0, 0))),
        ],
        axis=0,
    )

    def unpack(block):
        code = block[group_size : group_size + coded_rows].reshape(3, group_size).astype(jnp.int32)
        return (
            block[:group_size, :width].reshape(group_size, local_heads, HD),
            block[:group_size, width:].reshape(group_size, local_heads, HD),
            code[0] * 128 + code[1],
            code[2],
        )

    forward = RING[0]
    backward = [(b, a) for a, b in forward]

    def ring_step(state, _):
        carry, ahead, behind = state
        carry, _ = attend(carry, unpack(ahead))
        carry, _ = attend(carry, unpack(behind))
        ahead = lax.ppermute(ahead, "blk", forward)
        behind = lax.ppermute(behind, "blk", backward)
        return ((carry, ahead, behind), None)

    carry, _ = attend(initial, unpack(block))
    ahead = lax.ppermute(block, "blk", forward)
    behind = lax.ppermute(block, "blk", backward)
    (carry, ahead, behind), _ = lax.scan(
        ring_step, (carry, ahead, behind), None, length=n_blk // 2 - 2
    )
    opposite = lax.ppermute(ahead, "blk", forward)
    carry, _ = attend(carry, unpack(ahead))
    carry, _ = attend(carry, unpack(behind))
    carry, _ = attend(carry, unpack(opposite))
    highest, denom, summed = carry
    heads_out = (summed / denom[:, :, None]).astype(jnp.bfloat16)
    heads_out = jnp.transpose(heads_out, (1, 0, 2)).reshape(group_size, width)
    heads_local = lax.all_to_all(heads_out, EXP, split_axis=0, concat_axis=0, tiled=True)
    heads_local = jnp.transpose(
        heads_local.reshape(n_exp, local_rows, width), (1, 0, 2)
    ).reshape(local_rows, n_exp * width)
    attended = jnp.dot(heads_local, output_weight, preferred_element_type=jnp.float32)
    resid_local = (stream.astype(jnp.float32) + attended).astype(jnp.bfloat16)
    normed_local = rms_norm(resid_local, post_gain)
    normed_group = lax.all_gather(normed_local, EXP, axis=0, tiled=True)
    hidden = (
        jax.nn.silu(jnp.dot(normed_group, shared_gate, preferred_element_type=jnp.float32))
        * jnp.dot(normed_group, shared_up, preferred_element_type=jnp.float32)
    ).astype(jnp.bfloat16)
    opening = jax.nn.sigmoid(
        jnp.dot(normed_group, shared_router, preferred_element_type=jnp.float32)
    )
    shared_local = lax.psum_scatter(
        (
            jnp.dot(hidden, shared_down, preferred_element_type=jnp.float32) * opening[:, None]
        ).astype(jnp.bfloat16),
        EXP,
        scatter_dimension=0,
        tiled=True,
    ).astype(jnp.float32)
    experts = lax.axis_size(CHIPS)
    capacity = -(-max(2, 5 * local_rows * TOP // (4 * experts)) // 16) * 16
    flat_ids = expert_ids.reshape(-1)
    onehot = (flat_ids[:, None] == jnp.arange(experts, dtype=jnp.int32)[None, :]).astype(jnp.int32)
    slots = jnp.sum(onehot * (jnp.cumsum(onehot, axis=0) - 1), axis=1)
    target = flat_ids * capacity + slots
    slot_ids = jnp.arange(experts * capacity, dtype=jnp.int32)
    pick = jnp.any(
        (target[None, :] == slot_ids[:, None]).reshape(experts * capacity, local_rows, TOP), axis=2
    )
    outgoing = (
        jnp.dot(pick.astype(jnp.bfloat16), normed_local, preferred_element_type=jnp.float32)
        .astype(jnp.bfloat16)
        .reshape(experts, capacity, D)
    )
    arrived = lax.all_to_all(outgoing, CHIPS, split_axis=0, concat_axis=0, tiled=True)
    arrived = lax.all_gather(arrived, "core", axis=0)
    leading = arrived.shape[:-1]
    flat_rows = arrived.reshape(-1, D)
    hidden = (
        jax.nn.silu(jnp.dot(flat_rows, expert_gate[0], preferred_element_type=jnp.float32))
        * jnp.dot(flat_rows, expert_up[0], preferred_element_type=jnp.float32)
    ).astype(jnp.bfloat16)
    half_out = (
        jnp.dot(hidden, expert_down[0], preferred_element_type=jnp.float32)
        .astype(jnp.bfloat16)
        .reshape(leading + (D,))
    )
    core = lax.axis_index("core")
    own_half = lax.dynamic_index_in_dim(half_out, core, 0, keepdims=False)
    other_half = lax.ppermute(
        lax.dynamic_index_in_dim(half_out, 1 - core, 0, keepdims=False), "core", [(0, 1), (1, 0)]
    )
    summed_halves = (own_half.astype(jnp.float32) + other_half.astype(jnp.float32)).astype(
        jnp.bfloat16
    )
    returned = lax.all_to_all(summed_halves, CHIPS, split_axis=0, concat_axis=0, tiled=True)
    target_by_choice = target.reshape(local_rows, TOP).T.reshape(-1)
    gather_pick = (target_by_choice[:, None] == slot_ids[None, :]).astype(jnp.bfloat16)
    picked = jnp.dot(
        gather_pick, returned.reshape(-1, D), preferred_element_type=jnp.float32
    ) * route_weights.T.reshape(-1)[:, None]
    routed = jnp.sum(picked.reshape(TOP, local_rows, D), axis=0)
    final = (resid_local.astype(jnp.float32) + shared_local + routed).astype(jnp.bfloat16)
    return (final, cache_keys, cache_values)


def snake(mesh):
    blk = mesh.shape["blk"]
    try:
        spots = [tuple(mesh.devices.reshape(blk, -1)[b, 0].coords) for b in range(blk)]
        zs = sorted({s[2] for s in spots})
        order = []
        for i, z in enumerate(zs):
            row = sorted((b for b in range(blk) if spots[b][2] == z), key=lambda b: spots[b][1])
            order += row if i % 2 == 0 else row[::-1]
        assert sorted(order) == list(range(blk))
    except Exception:
        order = list(range(blk))
    return [(order[k], order[(k + 1) % blk]) for k in range(blk)]


def solution(mesh):
    blk, exp = mesh.shape["blk"], mesh.shape["exp"]
    chip_mesh = Mesh(mesh.devices.reshape(blk, exp // 2, 2), ("blk", "x", "core"))
    RING[0] = snake(mesh)
    rows = ("blk",) + EXP
    in_specs = (
        P(rows, None),
        P(),
        P(None, EXP),
        P(None, EXP),
        P(None, EXP),
        P(),
        P(),
        P(None, EXP),
        P(None, EXP),
        P(EXP, None),
        P(),
        P(rows, None, None),
        P(rows, None, None),
        P(rows, None, None),
        P(rows, None),
        P(rows, None),
        P(rows),
        P(rows),
        P(rows),
    )
    out_specs = (P(rows, None), P("blk", EXP), P("blk", EXP))
    return jax.shard_map(
        per_device, mesh=chip_mesh, in_specs=in_specs, out_specs=out_specs, check_vma=False
    )
```
